512 devices in a mesh: seq: 16 (over z, core), mlp: 8 (over y), tp: 4 (over x).
Axes of the slice: x: 4, y: 8, z: 8, core: 2. Of those that a mesh axis runs over, the one named last changes fastest.
Arguments:
- hidden: bfloat16 [64, 2048], P('mlp'), may hold values from -6 to 6
- lengths: int32 [64], P('mlp'), may hold values from 4 to 8192, as said below
- attention_gain: bfloat16 [2048], replicated, may hold values from 0.099609375 to 1.8984375
- query_weight: bfloat16 [2048, 2048], P('seq', 'tp'), may hold values from -0.125 to 0.125
- key_weight: bfloat16 [2048, 512], P('seq', 'tp'), may hold values from -0.125 to 0.125
- value_weight: bfloat16 [2048, 512], P('seq', 'tp'), may hold values from -0.125 to 0.125
- cached_keys: bfloat16 [64, 8192, 512], P('mlp', 'seq', 'tp'), may hold values from -800 to 800
- cached_values: bfloat16 [64, 8192, 512], P('mlp', 'seq', 'tp'), may hold values from -8 to 8
- output_weight: bfloat16 [2048, 2048], P('tp', 'seq'), may hold values from -0.125 to 0.125
- feedforward_gain: bfloat16 [2048], replicated, may hold values from 0.099609375 to 1.8984375
- gate_weight: bfloat16 [2048, 8192], P('mlp', ('seq', 'tp')), may hold values from -0.125 to 0.125
- up_weight: bfloat16 [2048, 8192], P('mlp', ('seq', 'tp')), may hold values from -0.125 to 0.125
- down_weight: bfloat16 [8192, 2048], P(('seq', 'tp'), 'mlp'), may hold values from -0.0625 to 0.0625
Outputs:
- updated_hidden: bfloat16 [64, 2048], P('mlp')
- new_keys: bfloat16 [64, 512], P('mlp', 'tp')
- new_values: bfloat16 [64, 512], P('mlp', 'tp')
The draws below stay inside these ranges and needn't reach their ends.
Inputs may be any that keep to these rules, and one draw needn't show every extreme that they name: `lengths`: one request in every draw has exactly 8192 cached tokens.
All inputs are finite; a program needn't handle non-finite values.
Results may differ from the reference program's by a relative error of at most 0.012.
Values may be sent and summed in bfloat16 or wider, within the bound.
No kernel may reach another device: no remote copies, remote signals or barrier semaphores. Data moves between devices by JAX's collectives and lax.ppermute only.
A program may use at most 64 MiB of HBM per device.

```python
import jax
import jax.numpy as jnp
from jax import lax

D = 2048
QH = 32
KVH = 8
HD = 64
FF = 8192
POS_DEV = 512
R = 64
MAXLEN = 8192


def draw_lengths(key, part):
    first_key, second_key = jax.random.split(key, 2)
    drawn = jax.random.randint(first_key, (R,), 4, MAXLEN + 1)
    chosen = jax.random.randint(second_key, (), 0, R)
    return jnp.where(jnp.arange(R) == chosen, MAXLEN, drawn).astype(jnp.int32)


def draw_cached_keys(key, part):
    first_key = jax.random.fold_in(key, 0)
    base_keys = jnp.clip(jax.random.normal(first_key, (R, MAXLEN, KVH * HD), jnp.float32), -5.0, 5.0)
    return base_keys.astype(jnp.bfloat16)


def draw_cached_values(key, part):
    first_key, second_key = jax.random.split(jax.random.fold_in(key, 7), 2)
    ramp = (jnp.arange(MAXLEN, dtype=jnp.float32) / MAXLEN).reshape(1, MAXLEN, 1)
    signs = jax.random.uniform(second_key, (R, 1, KVH * HD), jnp.float32, -1.0, 1.0)
    noise = jnp.clip(jax.random.normal(first_key, (R, MAXLEN, KVH * HD), jnp.float32), -5.0, 5.0)
    level = 0.5 + 1.5 * ramp
    return (noise + signs * level).astype(jnp.bfloat16)


def levels(stream_key, dims, cuts, least, high):
    def one(dim, blocks):
        heights = jax.random.uniform(jax.random.fold_in(jax.random.fold_in(stream_key, 6), dim), (blocks,), jnp.float32, least / len(cuts), high / len(cuts))
        return jnp.repeat(jnp.exp(heights), dims[dim] // blocks).reshape((-1,) + (1,) * (len(dims) - dim - 1))

    loudness = one(*cuts[0])
    for cut in cuts[1:]:
        loudness = loudness * one(*cut)
    return loudness


def centred(own_key, dims, spread, limit, cuts=(), held_as=jnp.bfloat16):
    array = spread * jax.random.normal(own_key, dims, jnp.float32)
    if cuts:
        array = array * levels(own_key, dims, cuts, -0.22, 0.18)
    return jnp.clip(array, -limit, limit).astype(held_as)


def setup_inputs(seed: int = 0) -> dict:
    seeds = jax.random.split(jax.random.key(seed), 14)
    hidden = centred(seeds[0], (R, D), 1.0, 6.0, ((0, 8),))
    lengths = draw_lengths(jax.random.fold_in(seeds[13], 71), 0)
    attention_gain = jnp.clip(1.0 + 0.18 * jax.random.normal(seeds[2], (D,), jnp.float32), 0.099609375, 1.8984375).astype(jnp.bfloat16)
    query_weight = centred(seeds[3], (D, QH * HD), D ** -0.5, 0.125, ((0, 16), (1, 4)))
    key_weight = centred(seeds[4], (D, KVH * HD), D ** -0.5, 0.125, ((0, 16), (1, 4)))
    value_weight = centred(seeds[5], (D, KVH * HD), D ** -0.5, 0.125, ((0, 16), (1, 4)))
    cached_keys = draw_cached_keys(jax.random.fold_in(seeds[13], 71), 0)
    cached_values = draw_cached_values(jax.random.fold_in(seeds[13], 71), 0)
    output_weight = centred(seeds[8], (QH * HD, D), (QH * HD) ** -0.5, 0.125, ((0, 4), (1, 16)))
    feedforward_gain = jnp.clip(1.0 + 0.18 * jax.random.normal(seeds[9], (D,), jnp.float32), 0.099609375, 1.8984375).astype(jnp.bfloat16)
    gate_weight = centred(seeds[10], (D, FF), D ** -0.5, 0.125, ((0, 8), (1, 64)))
    up_weight = centred(seeds[11], (D, FF), D ** -0.5, 0.125, ((0, 8), (1, 64)))
    down_weight = centred(seeds[12], (FF, D), FF ** -0.5, 0.0625, ((0, 64), (1, 8)))
    return dict(hidden=hidden, lengths=lengths, attention_gain=attention_gain, query_weight=query_weight, key_weight=key_weight, value_weight=value_weight, cached_keys=cached_keys, cached_values=cached_values, output_weight=output_weight, feedforward_gain=feedforward_gain, gate_weight=gate_weight, up_weight=up_weight, down_weight=down_weight)


def rms_norm(vectors, weights):
    mean_square = lax.optimization_barrier(jnp.mean(vectors * vectors, axis=-1, keepdims=True))
    return vectors * lax.rsqrt(mean_square + 1e-05) * weights.astype(jnp.float32)

def rotate(vectors, positions):
    half_dim = vectors.shape[-1] // 2
    inverse = 500000.0 ** (-(jnp.arange(half_dim, dtype=jnp.float32) * 2.0 / vectors.shape[-1]))
    angles = positions.astype(jnp.float32)[:, None] * inverse[None, :]
    cosine = jnp.cos(angles)[:, None, :]
    sine_part = jnp.sin(angles)[:, None, :]
    first_half = vectors[..., :half_dim]
    second_half = vectors[..., half_dim:]
    return jnp.concatenate([first_half * cosine - second_half * sine_part, second_half * cosine + first_half * sine_part], axis=-1)

def attend_one(operands):
    queries, key_new, value_new, keys_all, values_all, length = operands
    group_size = QH // KVH
    blocks = MAXLEN // POS_DEV
    score_scale = HD ** (-0.5)
    query_float = queries.astype(jnp.float32).reshape(KVH, group_size, HD)
    key_blocks = keys_all.astype(jnp.float32).reshape(blocks, POS_DEV, KVH, HD)
    value_blocks = values_all.astype(jnp.float32).reshape(blocks, POS_DEV, KVH, HD)
    scores = jnp.einsum('gqd,bpgd->bgqp', query_float, key_blocks) * score_scale
    position = jnp.arange(MAXLEN, dtype=jnp.int32).reshape(blocks, 1, 1, POS_DEV)
    valid_mask = position < length
    block_max = lax.optimization_barrier(jnp.max(jnp.where(valid_mask, scores, -1e+30), axis=-1))
    exp_weights = jnp.where(valid_mask, jnp.exp(scores - block_max[..., None]), 0.0)
    block_sum = lax.optimization_barrier(jnp.sum(exp_weights, axis=-1))
    rounded = lax.optimization_barrier(exp_weights.astype(jnp.bfloat16)).astype(jnp.float32)
    block_acc = jnp.einsum('bgqp,bpgd->bgqd', rounded, value_blocks)
    self_score = lax.optimization_barrier(jnp.sum(query_float * key_new.astype(jnp.float32).reshape(KVH, 1, HD), axis=-1)) * score_scale
    overall_max = jnp.maximum(lax.optimization_barrier(jnp.max(block_max, axis=0)), self_score)
    rescale = jnp.exp(block_max - overall_max)
    self_weight = jnp.exp(self_score - overall_max)
    total_weight = lax.optimization_barrier(jnp.sum(block_sum * rescale, axis=0)) + self_weight
    weighted_sum = lax.optimization_barrier(jnp.sum(block_acc * rescale[..., None], axis=0)) + self_weight[..., None] * value_new.astype(jnp.float32).reshape(KVH, 1, HD)
    return (weighted_sum / total_weight[..., None]).reshape(QH * HD).astype(jnp.bfloat16)

def reference(hidden, lengths, attention_gain, query_weight, key_weight, value_weight, cached_keys, cached_values, output_weight, feedforward_gain, gate_weight, up_weight, down_weight):
    stream = hidden.astype(jnp.float32)
    normed = rms_norm(stream, attention_gain).astype(jnp.bfloat16)
    queries_raw = jnp.dot(normed, query_weight, preferred_element_type=jnp.float32)
    keys_raw = jnp.dot(normed, key_weight, preferred_element_type=jnp.float32)
    values_raw = jnp.dot(normed, value_weight, preferred_element_type=jnp.float32)
    queries = rotate(queries_raw.reshape(R, QH, HD), lengths).reshape(R, QH * HD).astype(jnp.bfloat16)
    new_keys = rotate(keys_raw.reshape(R, KVH, HD), lengths).reshape(R, KVH * HD).astype(jnp.bfloat16)
    new_values = values_raw.astype(jnp.bfloat16)
    attended = lax.map(attend_one, (queries, new_keys, new_values, cached_keys, cached_values, lengths))
    projected = jnp.dot(attended, output_weight, preferred_element_type=jnp.float32).astype(jnp.bfloat16)
    mixed_stream = stream + lax.optimization_barrier(projected).astype(jnp.float32)
    mlp_input = rms_norm(mixed_stream, feedforward_gain).astype(jnp.bfloat16)
    gate = jnp.dot(mlp_input, gate_weight, preferred_element_type=jnp.float32)
    upward = jnp.dot(mlp_input, up_weight, preferred_element_type=jnp.float32)
    activated = (jax.nn.silu(gate) * upward).astype(jnp.bfloat16)
    down_out = jnp.dot(activated, down_weight, preferred_element_type=jnp.float32).astype(jnp.bfloat16)
    updated_hidden = (mixed_stream + lax.optimization_barrier(down_out).astype(jnp.float32)).astype(jnp.bfloat16)
    return (updated_hidden, new_keys, new_values)
```

```python
import jax
import jax.numpy as jnp
from jax import lax
from jax.sharding import PartitionSpec as P

HD = 64


def rms_norm(vectors, weights):
    mean_square = jnp.mean(vectors * vectors, axis=-1, keepdims=True)
    return vectors * lax.rsqrt(mean_square + 1e-05) * weights.astype(jnp.float32)


def rotate(vectors, positions):
    half_dim = vectors.shape[-1] // 2
    inverse = 500000.0 ** (-(jnp.arange(half_dim, dtype=jnp.float32) * 2.0 / vectors.shape[-1]))
    angles = positions.astype(jnp.float32)[:, None] * inverse[None, :]
    cosine = jnp.cos(angles)[:, None, :]
    sine_part = jnp.sin(angles)[:, None, :]
    first_half = vectors[..., :half_dim]
    second_half = vectors[..., half_dim:]
    return jnp.concatenate(
        [
            first_half * cosine - second_half * sine_part,
            second_half * cosine + first_half * sine_part,
        ],
        axis=-1,
    )


def gathered_sum(x, axis):
    return jnp.sum(lax.all_gather(x, axis), axis=0)


def butterfly_sum(x, axis):
    size = lax.axis_size(axis)
    step = 1
    while step < size:
        pairs = [(i, i ^ step) for i in range(size)]
        x = x + lax.ppermute(x, axis, pairs)
        step *= 2
    return x


def per_device(
    hidden,
    lengths,
    attention_gain,
    query_weight,
    key_weight,
    value_weight,
    cached_keys,
    cached_values,
    output_weight,
    feedforward_gain,
    gate_weight,
    up_weight,
    down_weight,
):
    hidden_units = gate_weight.shape[1]
    with jax.named_scope("mlp_weight_gather"):
        slab = jnp.concatenate([gate_weight, up_weight, down_weight.T], axis=1)
        full_slab = lax.all_gather(slab, "mlp", axis=0, tiled=True)
    gate_full = full_slab[:, :hidden_units]
    up_full = full_slab[:, hidden_units : 2 * hidden_units]
    down_full = full_slab[:, 2 * hidden_units :].T

    requests = hidden.shape[0]
    stream = hidden.astype(jnp.float32)
    normed = rms_norm(stream, attention_gain).astype(jnp.bfloat16)
    column_width = query_weight.shape[0]
    own_columns = lax.dynamic_slice_in_dim(
        normed, lax.axis_index("seq") * column_width, column_width, 1
    )
    query_width = query_weight.shape[1]
    key_width = key_weight.shape[1]
    with jax.named_scope("qkv_projection"):
        partial = jnp.concatenate(
            [
                jnp.dot(own_columns, query_weight, preferred_element_type=jnp.float32),
                jnp.dot(own_columns, key_weight, preferred_element_type=jnp.float32),
                jnp.dot(own_columns, value_weight, preferred_element_type=jnp.float32),
            ],
            axis=1,
        )
        total = gathered_sum(partial, "seq")
    queries_raw = total[:, :query_width]
    keys_raw = total[:, query_width : query_width + key_width]
    values_raw = total[:, query_width + key_width :]
    local_heads = query_width // HD
    key_heads = key_width // HD
    group_size = local_heads // key_heads
    queries = rotate(queries_raw.reshape(requests, local_heads, HD), lengths).astype(jnp.bfloat16)
    new_keys = (
        rotate(keys_raw.reshape(requests, key_heads, HD), lengths)
        .reshape(requests, key_heads * HD)
        .astype(jnp.bfloat16)
    )
    new_values = values_raw.astype(jnp.bfloat16)
    grouped = queries.reshape(requests, key_heads, group_size, HD)
    block_span = cached_keys.shape[1]
    key_blocks = cached_keys.reshape(requests, block_span, key_heads, HD)
    value_blocks = cached_values.reshape(requests, block_span, key_heads, HD)
    score_scale = HD ** (-0.5)
    first_position = lax.axis_index("seq") * block_span
    positions = first_position + jnp.arange(block_span, dtype=jnp.int32)
    valid_mask = (positions[None, :] < lengths[:, None])[:, None, None, :]
    with jax.named_scope("local_attention"):
        scores = (
            jnp.einsum("rgqd,rpgd->rgqp", grouped, key_blocks, preferred_element_type=jnp.float32)
            * score_scale
        )
        block_max = jnp.max(jnp.where(valid_mask, scores, -1e30), axis=-1)
        exp_weights = jnp.where(valid_mask, jnp.exp(scores - block_max[..., None]), 0.0)
        block_sum = jnp.sum(exp_weights, axis=-1)
        block_acc = jnp.einsum(
            "rgqp,rpgd->rgqd",
            exp_weights.astype(jnp.bfloat16),
            value_blocks,
            preferred_element_type=jnp.float32,
        )
    with jax.named_scope("softmax_merge"):
        state = jnp.concatenate([block_max[..., None], block_sum[..., None], block_acc], axis=-1)
        every_state = lax.all_gather(state, "seq")
        every_max = every_state[..., 0]
        every_sum = every_state[..., 1]
        every_acc = every_state[..., 2:]
        query_float = grouped.astype(jnp.float32)
        self_score = (
            jnp.sum(
                query_float * new_keys.astype(jnp.float32).reshape(requests, key_heads, 1, HD),
                axis=-1,
            )
            * score_scale
        )
        overall_max = jnp.maximum(jnp.max(every_max, axis=0), self_score)
        rescale = jnp.exp(every_max - overall_max[None])
        self_weight = jnp.exp(self_score - overall_max)
        total_weight = jnp.sum(every_sum * rescale, axis=0) + self_weight
        weighted_sum = jnp.sum(every_acc * rescale[..., None], axis=0) + self_weight[
            ..., None
        ] * new_values.astype(jnp.float32).reshape(requests, key_heads, 1, HD)
        attended = (
            (weighted_sum / total_weight[..., None])
            .reshape(requests, local_heads * HD)
            .astype(jnp.bfloat16)
        )
    with jax.named_scope("output_projection"):
        partial_output = jnp.dot(attended, output_weight, preferred_element_type=jnp.float32)
        projected = lax.psum(partial_output, "tp").astype(jnp.bfloat16)
        projected = lax.all_gather(projected, "seq", axis=1, tiled=True)
    mixed_stream = stream + projected.astype(jnp.float32)
    mlp_input = rms_norm(mixed_stream, feedforward_gain).astype(jnp.bfloat16)
    with jax.named_scope("feed_forward"):
        gate = jnp.dot(mlp_input, gate_full, preferred_element_type=jnp.float32)
        upward = jnp.dot(mlp_input, up_full, preferred_element_type=jnp.float32)
        activated = (jax.nn.silu(gate) * upward).astype(jnp.bfloat16)
        down_part = jnp.dot(activated, down_full, preferred_element_type=jnp.float32)
    with jax.named_scope("down_reduction"):
        down_total = butterfly_sum(butterfly_sum(down_part, "tp"), "seq").astype(jnp.bfloat16)
    updated_hidden = (mixed_stream + down_total.astype(jnp.float32)).astype(jnp.bfloat16)
    return (updated_hidden, new_keys, new_values)


def solution(mesh):
    return jax.shard_map(
        per_device,
        mesh=mesh,
        in_specs=(
            P("mlp", None),
            P("mlp"),
            P(),
            P("seq", "tp"),
            P("seq", "tp"),
            P("seq", "tp"),
            P("mlp", "seq", "tp"),
            P("mlp", "seq", "tp"),
            P("tp", "seq"),
            P(),
            P("mlp", ("seq", "tp")),
            P("mlp", ("seq", "tp")),
            P(("seq", "tp"), "mlp"),
        ),
        out_specs=(P("mlp", None), P("mlp", "tp"), P("mlp", "tp")),
        check_vma=False,
    )
```

```python
import jax
import jax.numpy as jnp
from jax import lax
from jax.sharding import PartitionSpec as P

HD = 64


def rms_norm(vectors, weights):
    mean_square = jnp.mean(vectors * vectors, axis=-1, keepdims=True)
    return vectors * lax.rsqrt(mean_square + 1e-05) * weights.astype(jnp.float32)


def rotate(vectors, positions):
    half_dim = vectors.shape[-1] // 2
    inverse = 500000.0 ** (-(jnp.arange(half_dim, dtype=jnp.float32) * 2.0 / vectors.shape[-1]))
    angles = positions.astype(jnp.float32)[:, None] * inverse[None, :]
    cosine = jnp.cos(angles)[:, None, :]
    sine_part = jnp.sin(angles)[:, None, :]
    first_half = vectors[..., :half_dim]
    second_half = vectors[..., half_dim:]
    return jnp.concatenate(
        [
            first_half * cosine - second_half * sine_part,
            second_half * cosine + first_half * sine_part,
        ],
        axis=-1,
    )


def gathered_sum(x, axis):
    return jnp.sum(lax.all_gather(x, axis), axis=0)


def gather_blocks(x, axis):
    size = lax.axis_size(axis)
    me = lax.axis_index(axis)
    held = x[None]
    step = 1
    while step < size:
        other = lax.ppermute(held, axis, [(i, i ^ step) for i in range(size)])
        upper = (me // step) % 2 == 1
        held = jnp.where(
            upper,
            jnp.concatenate([other, held], axis=0),
            jnp.concatenate([held, other], axis=0),
        )
        step *= 2
    return held


def butterfly_sum(x, axis):
    size = lax.axis_size(axis)
    step = 1
    while step < size:
        pairs = [(i, i ^ step) for i in range(size)]
        x = x + lax.ppermute(x, axis, pairs)
        step *= 2
    return x


def per_device(
    hidden,
    lengths,
    attention_gain,
    query_weight,
    key_weight,
    value_weight,
    cached_keys,
    cached_values,
    output_weight,
    feedforward_gain,
    gate_weight,
    up_weight,
    down_weight,
):
    slab_rows, hidden_units = gate_weight.shape
    with jax.named_scope("mlp_weight_gather"):
        slab = jnp.stack(
            [gate_weight, up_weight, down_weight.reshape(slab_rows, hidden_units)], axis=0
        )
        blocks = gather_blocks(slab, "mlp")
    slabs = blocks.shape[0]
    gate_full = blocks[:, 0].reshape(slabs * slab_rows, hidden_units)
    up_full = blocks[:, 1].reshape(slabs * slab_rows, hidden_units)
    down_blocks = blocks[:, 2].reshape(slabs, hidden_units, slab_rows)

    requests = hidden.shape[0]
    stream = hidden.astype(jnp.float32)
    normed = rms_norm(stream, attention_gain).astype(jnp.bfloat16)
    column_width = query_weight.shape[0]
    own_columns = lax.dynamic_slice_in_dim(
        normed, lax.axis_index("seq") * column_width, column_width, 1
    )
    query_width = query_weight.shape[1]
    key_width = key_weight.shape[1]
    with jax.named_scope("qkv_projection"):
        partial = jnp.concatenate(
            [
                jnp.dot(own_columns, query_weight, preferred_element_type=jnp.float32),
                jnp.dot(own_columns, key_weight, preferred_element_type=jnp.float32),
                jnp.dot(own_columns, value_weight, preferred_element_type=jnp.float32),
            ],
            axis=1,
        )
        total = gathered_sum(partial, "seq")
    queries_raw = total[:, :query_width]
    keys_raw = total[:, query_width : query_width + key_width]
    values_raw = total[:, query_width + key_width :]
    local_heads = query_width // HD
    key_heads = key_width // HD
    group_size = local_heads // key_heads
    queries = rotate(queries_raw.reshape(requests, local_heads, HD), lengths).astype(jnp.bfloat16)
    new_keys = (
        rotate(keys_raw.reshape(requests, key_heads, HD), lengths)
        .reshape(requests, key_heads * HD)
        .astype(jnp.bfloat16)
    )
    new_values = values_raw.astype(jnp.bfloat16)
    grouped = queries.reshape(requests, key_heads, group_size, HD)
    block_span = cached_keys.shape[1]
    key_blocks = cached_keys.reshape(requests, block_span, key_heads, HD)
    value_blocks = cached_values.reshape(requests, block_span, key_heads, HD)
    score_scale = HD ** (-0.5)
    first_position = lax.axis_index("seq") * block_span
    positions = first_position + jnp.arange(block_span, dtype=jnp.int32)
    valid_mask = (positions[None, :] < lengths[:, None])[:, None, None, :]
    with jax.named_scope("local_attention"):
        scores = (
            jnp.einsum("rgqd,rpgd->rgqp", grouped, key_blocks, preferred_element_type=jnp.float32)
            * score_scale
        )
        block_max = jnp.max(jnp.where(valid_mask, scores, -1e30), axis=-1)
        exp_weights = jnp.where(valid_mask, jnp.exp(scores - block_max[..., None]), 0.0)
        block_sum = jnp.sum(exp_weights, axis=-1)
        block_acc = jnp.einsum(
            "rgqp,rpgd->rgqd",
            exp_weights.astype(jnp.bfloat16),
            value_blocks,
            preferred_element_type=jnp.float32,
        )
    with jax.named_scope("softmax_merge"):
        state = jnp.concatenate([block_max[..., None], block_sum[..., None], block_acc], axis=-1)
        every_state = lax.all_gather(state, "seq")
        every_max = every_state[..., 0]
        every_sum = every_state[..., 1]
        every_acc = every_state[..., 2:]
        query_float = grouped.astype(jnp.float32)
        self_score = (
            jnp.sum(
                query_float * new_keys.astype(jnp.float32).reshape(requests, key_heads, 1, HD),
                axis=-1,
            )
            * score_scale
        )
        overall_max = jnp.maximum(jnp.max(every_max, axis=0), self_score)
        rescale = jnp.exp(every_max - overall_max[None])
        self_weight = jnp.exp(self_score - overall_max)
        total_weight = jnp.sum(every_sum * rescale, axis=0) + self_weight
        weighted_sum = jnp.sum(every_acc * rescale[..., None], axis=0) + self_weight[
            ..., None
        ] * new_values.astype(jnp.float32).reshape(requests, key_heads, 1, HD)
        attended = (
            (weighted_sum / total_weight[..., None])
            .reshape(requests, local_heads * HD)
            .astype(jnp.bfloat16)
        )
    with jax.named_scope("output_projection"):
        partial_output = jnp.dot(attended, output_weight, preferred_element_type=jnp.float32)
        projected = lax.psum(partial_output, "tp").astype(jnp.bfloat16)
        projected = lax.all_gather(projected, "seq", axis=1, tiled=True)
    mixed_stream = stream + projected.astype(jnp.float32)
    mlp_input = rms_norm(mixed_stream, feedforward_gain).astype(jnp.bfloat16)
    with jax.named_scope("feed_forward"):
        gate = jnp.dot(mlp_input, gate_full, preferred_element_type=jnp.float32)
        upward = jnp.dot(mlp_input, up_full, preferred_element_type=jnp.float32)
        activated = (jax.nn.silu(gate) * upward).astype(jnp.bfloat16)
        down_part = jnp.einsum(
            "rh,jhc->rjc", activated, down_blocks, preferred_element_type=jnp.float32
        ).reshape(requests, slabs * slab_rows)
    with jax.named_scope("down_reduction"):
        down_total = butterfly_sum(gathered_sum(down_part, "tp"), "seq").astype(jnp.bfloat16)
    updated_hidden = (mixed_stream + down_total.astype(jnp.float32)).astype(jnp.bfloat16)
    return (updated_hidden, new_keys, new_values)


def solution(mesh):
    return jax.shard_map(
        per_device,
        mesh=mesh,
        in_specs=(
            P("mlp", None),
            P("mlp"),
            P(),
            P("seq", "tp"),
            P("seq", "tp"),
            P("seq", "tp"),
            P("mlp", "seq", "tp"),
            P("mlp", "seq", "tp"),
            P("tp", "seq"),
            P(),
            P("mlp", ("seq", "tp")),
            P("mlp", ("seq", "tp")),
            P(("seq", "tp"), "mlp"),
        ),
        out_specs=(P("mlp", None), P("mlp", "tp"), P("mlp", "tp")),
        check_vma=False,
    )
```

```python
import jax
import jax.numpy as jnp
from jax import lax
from jax.sharding import PartitionSpec as P

HD = 64


def rms_norm(vectors, weights):
    mean_square = jnp.mean(vectors * vectors, axis=-1, keepdims=True)
    return vectors * lax.rsqrt(mean_square + 1e-05) * weights.astype(jnp.float32)


def rotate(vectors, positions):
    half_dim = vectors.shape[-1] // 2
    inverse = 500000.0 ** (-(jnp.arange(half_dim, dtype=jnp.float32) * 2.0 / vectors.shape[-1]))
    angles = positions.astype(jnp.float32)[:, None] * inverse[None, :]
    cosine = jnp.cos(angles)[:, None, :]
    sine_part = jnp.sin(angles)[:, None, :]
    first_half = vectors[..., :half_dim]
    second_half = vectors[..., half_dim:]
    return jnp.concatenate(
        [
            first_half * cosine - second_half * sine_part,
            second_half * cosine + first_half * sine_part,
        ],
        axis=-1,
    )


def gathered_sum(x, axis):
    return jnp.sum(lax.all_gather(x, axis), axis=0)


def gather_by_exchange(x, axes):
    count = 1
    for axis in axes:
        count *= lax.axis_size(axis)
    copies = jnp.broadcast_to(x[None], (count,) + x.shape)
    return lax.all_to_all(copies, axes, 0, 0, tiled=True)


def per_device(
    hidden,
    lengths,
    attention_gain,
    query_weight,
    key_weight,
    value_weight,
    cached_keys,
    cached_values,
    output_weight,
    feedforward_gain,
    gate_weight,
    up_weight,
    down_weight,
):
    slab_rows, hidden_units = gate_weight.shape
    with jax.named_scope("mlp_weight_gather"):
        slab = jnp.stack(
            [gate_weight, up_weight, down_weight.reshape(slab_rows, hidden_units)], axis=0
        )
        blocks = lax.all_gather(slab, "mlp")
    slabs = blocks.shape[0]
    gate_full = blocks[:, 0].reshape(slabs * slab_rows, hidden_units)
    up_full = blocks[:, 1].reshape(slabs * slab_rows, hidden_units)
    down_blocks = blocks[:, 2].reshape(slabs, hidden_units, slab_rows)

    requests = hidden.shape[0]
    stream = hidden.astype(jnp.float32)
    normed = rms_norm(stream, attention_gain).astype(jnp.bfloat16)
    column_width = query_weight.shape[0]
    own_columns = lax.dynamic_slice_in_dim(
        normed, lax.axis_index("seq") * column_width, column_width, 1
    )
    query_width = query_weight.shape[1]
    key_width = key_weight.shape[1]
    with jax.named_scope("qkv_projection"):
        partial = jnp.concatenate(
            [
                jnp.dot(own_columns, query_weight, preferred_element_type=jnp.float32),
                jnp.dot(own_columns, key_weight, preferred_element_type=jnp.float32),
                jnp.dot(own_columns, value_weight, preferred_element_type=jnp.float32),
            ],
            axis=1,
        )
        total = gathered_sum(partial, "seq")
    queries_raw = total[:, :query_width]
    keys_raw = total[:, query_width : query_width + key_width]
    values_raw = total[:, query_width + key_width :]
    local_heads = query_width // HD
    key_heads = key_width // HD
    group_size = local_heads // key_heads
    queries = rotate(queries_raw.reshape(requests, local_heads, HD), lengths).astype(jnp.bfloat16)
    new_keys = (
        rotate(keys_raw.reshape(requests, key_heads, HD), lengths)
        .reshape(requests, key_heads * HD)
        .astype(jnp.bfloat16)
    )
    new_values = values_raw.astype(jnp.bfloat16)
    grouped = queries.reshape(requests, key_heads, group_size, HD)
    block_span = cached_keys.shape[1]
    key_blocks = cached_keys.reshape(requests, block_span, key_heads, HD)
    value_blocks = cached_values.reshape(requests, block_span, key_heads, HD)
    score_scale = HD ** (-0.5)
    first_position = lax.axis_index("seq") * block_span
    positions = first_position + jnp.arange(block_span, dtype=jnp.int32)
    valid_mask = (positions[None, :] < lengths[:, None])[:, None, None, :]
    with jax.named_scope("local_attention"):
        scores = (
            jnp.einsum("rgqd,rpgd->rgqp", grouped, key_blocks, preferred_element_type=jnp.float32)
            * score_scale
        )
        block_max = jnp.max(jnp.where(valid_mask, scores, -1e30), axis=-1)
        exp_weights = jnp.where(valid_mask, jnp.exp(scores - block_max[..., None]), 0.0)
        block_sum = jnp.sum(exp_weights, axis=-1)
        block_acc = jnp.einsum(
            "rgqp,rpgd->rgqd",
            exp_weights.astype(jnp.bfloat16),
            value_blocks,
            preferred_element_type=jnp.float32,
        )
    with jax.named_scope("softmax_merge"):
        state = jnp.concatenate([block_max[..., None], block_sum[..., None], block_acc], axis=-1)
        every_state = lax.all_gather(state, "seq")
        every_max = every_state[..., 0]
        every_sum = every_state[..., 1]
        every_acc = every_state[..., 2:]
        query_float = grouped.astype(jnp.float32)
        self_score = (
            jnp.sum(
                query_float * new_keys.astype(jnp.float32).reshape(requests, key_heads, 1, HD),
                axis=-1,
            )
            * score_scale
        )
        overall_max = jnp.maximum(jnp.max(every_max, axis=0), self_score)
        rescale = jnp.exp(every_max - overall_max[None])
        self_weight = jnp.exp(self_score - overall_max)
        total_weight = jnp.sum(every_sum * rescale, axis=0) + self_weight
        weighted_sum = jnp.sum(every_acc * rescale[..., None], axis=0) + self_weight[
            ..., None
        ] * new_values.astype(jnp.float32).reshape(requests, key_heads, 1, HD)
        attended = (
            (weighted_sum / total_weight[..., None])
            .reshape(requests, local_heads * HD)
            .astype(jnp.bfloat16)
        )
    with jax.named_scope("output_projection"):
        partial_output = jnp.dot(attended, output_weight, preferred_element_type=jnp.float32)
        every_partial = gather_by_exchange(partial_output.astype(jnp.bfloat16), ("seq", "tp"))
        column_blocks = lax.axis_size("seq")
        projected = (
            every_partial.reshape(column_blocks, lax.axis_size("tp"), requests, -1)
            .astype(jnp.float32)
            .sum(axis=1)
            .astype(jnp.bfloat16)
            .transpose(1, 0, 2)
            .reshape(requests, -1)
        )
    mixed_stream = stream + projected.astype(jnp.float32)
    mlp_input = rms_norm(mixed_stream, feedforward_gain).astype(jnp.bfloat16)
    with jax.named_scope("feed_forward"):
        gate = jnp.dot(mlp_input, gate_full, preferred_element_type=jnp.float32)
        upward = jnp.dot(mlp_input, up_full, preferred_element_type=jnp.float32)
        activated = (jax.nn.silu(gate) * upward).astype(jnp.bfloat16)
        down_part = jnp.einsum(
            "rh,jhc->rjc", activated, down_blocks, preferred_element_type=jnp.float32
        ).reshape(requests, slabs * slab_rows)
    with jax.named_scope("down_reduction"):
        reducers = lax.axis_size("seq") * lax.axis_size("tp")
        pieces = down_part.reshape(requests, reducers, -1).transpose(1, 0, 2)
        own_piece = lax.all_to_all(pieces, ("seq", "tp"), 0, 0, tiled=True).sum(axis=0)
        every_piece = gather_by_exchange(own_piece.astype(jnp.bfloat16), ("seq", "tp"))
        down_total = every_piece.transpose(1, 0, 2).reshape(requests, -1)
    updated_hidden = (mixed_stream + down_total.astype(jnp.float32)).astype(jnp.bfloat16)
    return (updated_hidden, new_keys, new_values)


def solution(mesh):
    return jax.shard_map(
        per_device,
        mesh=mesh,
        in_specs=(
            P("mlp", None),
            P("mlp"),
            P(),
            P("seq", "tp"),
            P("seq", "tp"),
            P("seq", "tp"),
            P("mlp", "seq", "tp"),
            P("mlp", "seq", "tp"),
            P("tp", "seq"),
            P(),
            P("mlp", ("seq", "tp")),
            P("mlp", ("seq", "tp")),
            P(("seq", "tp"), "mlp"),
        ),
        out_specs=(P("mlp", None), P("mlp", "tp"), P("mlp", "tp")),
        check_vma=False,
    )
```

```python
import jax
import jax.numpy as jnp
from jax import lax
from jax.sharding import PartitionSpec as P

HD = 64


def rms_norm(vectors, weights):
    mean_square = jnp.mean(vectors * vectors, axis=-1, keepdims=True)
    return vectors * lax.rsqrt(mean_square + 1e-05) * weights.astype(jnp.float32)


def rotate(vectors, positions):
    half_dim = vectors.shape[-1] // 2
    inverse = 500000.0 ** (-(jnp.arange(half_dim, dtype=jnp.float32) * 2.0 / vectors.shape[-1]))
    angles = positions.astype(jnp.float32)[:, None] * inverse[None, :]
    cosine = jnp.cos(angles)[:, None, :]
    sine_part = jnp.sin(angles)[:, None, :]
    first_half = vectors[..., :half_dim]
    second_half = vectors[..., half_dim:]
    return jnp.concatenate(
        [
            first_half * cosine - second_half * sine_part,
            second_half * cosine + first_half * sine_part,
        ],
        axis=-1,
    )


def gathered_sum(x, axis):
    return jnp.sum(lax.all_gather(x, axis), axis=0)


def gather_by_exchange(x, axes):
    count = 1
    for axis in axes:
        count *= lax.axis_size(axis)
    copies = jnp.broadcast_to(x[None], (count,) + x.shape)
    return lax.all_to_all(copies, axes, 0, 0, tiled=True)


def per_device(
    hidden,
    lengths,
    attention_gain,
    query_weight,
    key_weight,
    value_weight,
    cached_keys,
    cached_values,
    output_weight,
    feedforward_gain,
    gate_weight,
    up_weight,
    down_weight,
):
    slab_rows, hidden_units = gate_weight.shape
    with jax.named_scope("mlp_weight_gather"):
        slab = jnp.concatenate(
            [jnp.concatenate([gate_weight, up_weight], axis=1), down_weight], axis=0
        )
        blocks = lax.all_gather(slab, "mlp")
    slabs = blocks.shape[0]
    gate_full = blocks[:, :slab_rows, :hidden_units].reshape(slabs * slab_rows, hidden_units)
    up_full = blocks[:, :slab_rows, hidden_units:].reshape(slabs * slab_rows, hidden_units)
    down_blocks = blocks[:, slab_rows:, :]

    requests = hidden.shape[0]
    stream = hidden.astype(jnp.float32)
    normed = rms_norm(stream, attention_gain).astype(jnp.bfloat16)
    column_width = query_weight.shape[0]
    own_columns = lax.dynamic_slice_in_dim(
        normed, lax.axis_index("seq") * column_width, column_width, 1
    )
    query_width = query_weight.shape[1]
    key_width = key_weight.shape[1]
    with jax.named_scope("qkv_projection"):
        partial = jnp.concatenate(
            [
                jnp.dot(own_columns, query_weight, preferred_element_type=jnp.float32),
                jnp.dot(own_columns, key_weight, preferred_element_type=jnp.float32),
                jnp.dot(own_columns, value_weight, preferred_element_type=jnp.float32),
            ],
            axis=1,
        )
        total = gathered_sum(partial, "seq")
    queries_raw = total[:, :query_width]
    keys_raw = total[:, query_width : query_width + key_width]
    values_raw = total[:, query_width + key_width :]
    local_heads = query_width // HD
    key_heads = key_width // HD
    group_size = local_heads // key_heads
    queries = rotate(queries_raw.reshape(requests, local_heads, HD), lengths).astype(jnp.bfloat16)
    new_keys = (
        rotate(keys_raw.reshape(requests, key_heads, HD), lengths)
        .reshape(requests, key_heads * HD)
        .astype(jnp.bfloat16)
    )
    new_values = values_raw.astype(jnp.bfloat16)
    grouped = queries.reshape(requests, key_heads, group_size, HD)
    block_span = cached_keys.shape[1]
    key_blocks = cached_keys.reshape(requests, block_span, key_heads, HD)
    value_blocks = cached_values.reshape(requests, block_span, key_heads, HD)
    score_scale = HD ** (-0.5)
    first_position = lax.axis_index("seq") * block_span
    positions = first_position + jnp.arange(block_span, dtype=jnp.int32)
    valid_mask = (positions[None, :] < lengths[:, None])[:, None, None, :]
    with jax.named_scope("local_attention"):
        scores = (
            jnp.einsum("rgqd,rpgd->rgqp", grouped, key_blocks, preferred_element_type=jnp.float32)
            * score_scale
        )
        block_max = jnp.max(jnp.where(valid_mask, scores, -1e30), axis=-1)
        exp_weights = jnp.where(valid_mask, jnp.exp(scores - block_max[..., None]), 0.0)
        block_sum = jnp.sum(exp_weights, axis=-1)
        block_acc = jnp.einsum(
            "rgqp,rpgd->rgqd",
            exp_weights.astype(jnp.bfloat16),
            value_blocks,
            preferred_element_type=jnp.float32,
        )
    with jax.named_scope("softmax_merge"):
        state = jnp.concatenate([block_max[..., None], block_sum[..., None], block_acc], axis=-1)
        every_state = lax.all_gather(state, "seq")
        every_max = every_state[..., 0]
        every_sum = every_state[..., 1]
        every_acc = every_state[..., 2:]
        query_float = grouped.astype(jnp.float32)
        self_score = (
            jnp.sum(
                query_float * new_keys.astype(jnp.float32).reshape(requests, key_heads, 1, HD),
                axis=-1,
            )
            * score_scale
        )
        overall_max = jnp.maximum(jnp.max(every_max, axis=0), self_score)
        rescale = jnp.exp(every_max - overall_max[None])
        self_weight = jnp.exp(self_score - overall_max)
        total_weight = jnp.sum(every_sum * rescale, axis=0) + self_weight
        weighted_sum = jnp.sum(every_acc * rescale[..., None], axis=0) + self_weight[
            ..., None
        ] * new_values.astype(jnp.float32).reshape(requests, key_heads, 1, HD)
        attended = (
            (weighted_sum / total_weight[..., None])
            .reshape(requests, local_heads * HD)
            .astype(jnp.bfloat16)
        )
    with jax.named_scope("output_projection"):
        partial_output = jnp.dot(attended, output_weight, preferred_element_type=jnp.float32)
        every_partial = gather_by_exchange(partial_output.astype(jnp.bfloat16), ("seq", "tp"))
        column_blocks = lax.axis_size("seq")
        projected = (
            every_partial.reshape(column_blocks, lax.axis_size("tp"), requests, -1)
            .astype(jnp.float32)
            .sum(axis=1)
            .astype(jnp.bfloat16)
            .transpose(1, 0, 2)
            .reshape(requests, -1)
        )
    mixed_stream = stream + projected.astype(jnp.float32)
    mlp_input = rms_norm(mixed_stream, feedforward_gain).astype(jnp.bfloat16)
    with jax.named_scope("feed_forward"):
        gate = jnp.dot(mlp_input, gate_full, preferred_element_type=jnp.float32)
        upward = jnp.dot(mlp_input, up_full, preferred_element_type=jnp.float32)
        activated = (jax.nn.silu(gate) * upward).astype(jnp.bfloat16)
        down_part = jnp.einsum(
            "rh,jhc->rjc", activated, down_blocks, preferred_element_type=jnp.float32
        ).reshape(requests, slabs * slab_rows)
    with jax.named_scope("down_reduction"):
        reducers = lax.axis_size("seq") * lax.axis_size("tp")
        pieces = down_part.reshape(requests, reducers, -1).transpose(1, 0, 2)
        own_piece = lax.all_to_all(pieces, ("seq", "tp"), 0, 0, tiled=True).sum(axis=0)
        every_piece = gather_by_exchange(own_piece.astype(jnp.bfloat16), ("seq", "tp"))
        down_total = every_piece.transpose(1, 0, 2).reshape(requests, -1)
    updated_hidden = (mixed_stream + down_total.astype(jnp.float32)).astype(jnp.bfloat16)
    return (updated_hidden, new_keys, new_values)


def solution(mesh):
    return jax.shard_map(
        per_device,
        mesh=mesh,
        in_specs=(
            P("mlp", None),
            P("mlp"),
            P(),
            P("seq", "tp"),
            P("seq", "tp"),
            P("seq", "tp"),
            P("mlp", "seq", "tp"),
            P("mlp", "seq", "tp"),
            P("tp", "seq"),
            P(),
            P("mlp", ("seq", "tp")),
            P("mlp", ("seq", "tp")),
            P(("seq", "tp"), "mlp"),
        ),
        out_specs=(P("mlp", None), P("mlp", "tp"), P("mlp", "tp")),
        check_vma=False,
    )
```

```python
import jax
import jax.numpy as jnp
from jax import lax
from jax.sharding import PartitionSpec as P

HD = 64


def rms_norm(vectors, weights):
    mean_square = jnp.mean(vectors * vectors, axis=-1, keepdims=True)
    return vectors * lax.rsqrt(mean_square + 1e-05) * weights.astype(jnp.float32)


def rotate(vectors, positions):
    half_dim = vectors.shape[-1] // 2
    inverse = 500000.0 ** (-(jnp.arange(half_dim, dtype=jnp.float32) * 2.0 / vectors.shape[-1]))
    angles = positions.astype(jnp.float32)[:, None] * inverse[None, :]
    cosine = jnp.cos(angles)[:, None, :]
    sine_part = jnp.sin(angles)[:, None, :]
    first_half = vectors[..., :half_dim]
    second_half = vectors[..., half_dim:]
    return jnp.concatenate(
        [
            first_half * cosine - second_half * sine_part,
            second_half * cosine + first_half * sine_part,
        ],
        axis=-1,
    )


def gathered_sum(x, axis):
    return jnp.sum(lax.all_gather(x, axis), axis=0)


def gather_by_exchange(x, axes):
    count = 1
    for axis in axes:
        count *= lax.axis_size(axis)
    copies = jnp.broadcast_to(x[None], (count,) + x.shape)
    return lax.all_to_all(copies, axes, 0, 0, tiled=True)


def per_device(
    hidden,
    lengths,
    attention_gain,
    query_weight,
    key_weight,
    value_weight,
    cached_keys,
    cached_values,
    output_weight,
    feedforward_gain,
    gate_weight,
    up_weight,
    down_weight,
):
    slab_rows, hidden_units = gate_weight.shape
    with jax.named_scope("mlp_weight_gather"):
        slab = jnp.concatenate(
            [jnp.concatenate([gate_weight, up_weight], axis=1), down_weight], axis=0
        )
        blocks = lax.all_gather(slab, "mlp")
    slabs = blocks.shape[0]
    gate_full = blocks[:, :slab_rows, :hidden_units].reshape(slabs * slab_rows, hidden_units)
    up_full = blocks[:, :slab_rows, hidden_units:].reshape(slabs * slab_rows, hidden_units)
    down_blocks = blocks[:, slab_rows:, :]

    requests = hidden.shape[0]
    stream = hidden.astype(jnp.float32)
    normed = rms_norm(stream, attention_gain).astype(jnp.bfloat16)
    column_width = query_weight.shape[0]
    own_columns = lax.dynamic_slice_in_dim(
        normed, lax.axis_index("seq") * column_width, column_width, 1
    )
    query_width = query_weight.shape[1]
    key_width = key_weight.shape[1]
    with jax.named_scope("qkv_projection"):
        partial = jnp.concatenate(
            [
                jnp.dot(own_columns, query_weight, preferred_element_type=jnp.float32),
                jnp.dot(own_columns, key_weight, preferred_element_type=jnp.float32),
                jnp.dot(own_columns, value_weight, preferred_element_type=jnp.float32),
            ],
            axis=1,
        )
        total = gathered_sum(partial, "seq")
    queries_raw = total[:, :query_width]
    keys_raw = total[:, query_width : query_width + key_width]
    values_raw = total[:, query_width + key_width :]
    local_heads = query_width // HD
    key_heads = key_width // HD
    group_size = local_heads // key_heads
    queries = rotate(queries_raw.reshape(requests, local_heads, HD), lengths).astype(jnp.bfloat16)
    new_keys = (
        rotate(keys_raw.reshape(requests, key_heads, HD), lengths)
        .reshape(requests, key_heads * HD)
        .astype(jnp.bfloat16)
    )
    new_values = values_raw.astype(jnp.bfloat16)
    grouped = queries.reshape(requests, key_heads, group_size, HD)
    block_span = cached_keys.shape[1]
    score_scale = HD ** (-0.5)
    first_position = lax.axis_index("seq") * block_span
    positions = first_position + jnp.arange(block_span, dtype=jnp.int32)
    valid_mask = (positions[None, :] < lengths[:, None])[:, None, :]
    own_head = jnp.arange(key_heads)[:, None] == jnp.arange(key_heads)[None, :]
    with jax.named_scope("local_attention"):
        padded_queries = jnp.where(
            own_head[None, :, None, :, None],
            grouped[:, :, :, None, :],
            jnp.zeros((), grouped.dtype),
        ).reshape(requests, key_heads * group_size, key_heads * HD)
        scores = (
            jnp.einsum(
                "rmk,rpk->rmp", padded_queries, cached_keys, preferred_element_type=jnp.float32
            )
            * score_scale
        )
        block_max = jnp.max(jnp.where(valid_mask, scores, -1e30), axis=-1)
        exp_weights = jnp.where(valid_mask, jnp.exp(scores - block_max[..., None]), 0.0)
        block_sum = jnp.sum(exp_weights, axis=-1)
        every_head_acc = jnp.einsum(
            "rmp,rpk->rmk",
            exp_weights.astype(jnp.bfloat16),
            cached_values,
            preferred_element_type=jnp.float32,
        ).reshape(requests, key_heads * group_size, key_heads, HD)
        own_block = jnp.repeat(own_head, group_size, axis=0)
        block_acc = jnp.sum(jnp.where(own_block[None, :, :, None], every_head_acc, 0.0), axis=2)
    with jax.named_scope("softmax_merge"):
        state = jnp.concatenate([block_max[..., None], block_sum[..., None], block_acc], axis=-1)
        every_state = lax.all_gather(state, "seq")
        every_max = every_state[..., 0]
        every_sum = every_state[..., 1]
        every_acc = every_state[..., 2:]
        query_float = grouped.astype(jnp.float32).reshape(requests, local_heads, HD)
        head_keys = jnp.repeat(
            new_keys.astype(jnp.float32).reshape(requests, key_heads, HD), group_size, axis=1
        )
        head_values = jnp.repeat(
            new_values.astype(jnp.float32).reshape(requests, key_heads, HD), group_size, axis=1
        )
        self_score = jnp.sum(query_float * head_keys, axis=-1) * score_scale
        overall_max = jnp.maximum(jnp.max(every_max, axis=0), self_score)
        rescale = jnp.exp(every_max - overall_max[None])
        self_weight = jnp.exp(self_score - overall_max)
        total_weight = jnp.sum(every_sum * rescale, axis=0) + self_weight
        weighted_sum = (
            jnp.sum(every_acc * rescale[..., None], axis=0) + self_weight[..., None] * head_values
        )
        attended = (
            (weighted_sum / total_weight[..., None])
            .reshape(requests, local_heads * HD)
            .astype(jnp.bfloat16)
        )
    with jax.named_scope("output_projection"):
        partial_output = jnp.dot(attended, output_weight, preferred_element_type=jnp.float32)
        every_partial = gather_by_exchange(partial_output.astype(jnp.bfloat16), ("seq", "tp"))
        column_blocks = lax.axis_size("seq")
        projected = (
            every_partial.reshape(column_blocks, lax.axis_size("tp"), requests, -1)
            .astype(jnp.float32)
            .sum(axis=1)
            .astype(jnp.bfloat16)
            .transpose(1, 0, 2)
            .reshape(requests, -1)
        )
    mixed_stream = stream + projected.astype(jnp.float32)
    mlp_input = rms_norm(mixed_stream, feedforward_gain).astype(jnp.bfloat16)
    with jax.named_scope("feed_forward"):
        gate = jnp.dot(mlp_input, gate_full, preferred_element_type=jnp.float32)
        upward = jnp.dot(mlp_input, up_full, preferred_element_type=jnp.float32)
        activated = (jax.nn.silu(gate) * upward).astype(jnp.bfloat16)
        down_part = jnp.einsum(
            "rh,jhc->rjc", activated, down_blocks, preferred_element_type=jnp.float32
        ).reshape(requests, slabs * slab_rows)
    with jax.named_scope("down_reduction"):
        reducers = lax.axis_size("seq") * lax.axis_size("tp")
        pieces = down_part.reshape(requests, reducers, -1).transpose(1, 0, 2)
        own_piece = lax.all_to_all(pieces, ("seq", "tp"), 0, 0, tiled=True).sum(axis=0)
        every_piece = gather_by_exchange(own_piece.astype(jnp.bfloat16), ("seq", "tp"))
        down_total = every_piece.transpose(1, 0, 2).reshape(requests, -1)
    updated_hidden = (mixed_stream + down_total.astype(jnp.float32)).astype(jnp.bfloat16)
    return (updated_hidden, new_keys, new_values)


def solution(mesh):
    return jax.shard_map(
        per_device,
        mesh=mesh,
        in_specs=(
            P("mlp", None),
            P("mlp"),
            P(),
            P("seq", "tp"),
            P("seq", "tp"),
            P("seq", "tp"),
            P("mlp", "seq", "tp"),
            P("mlp", "seq", "tp"),
            P("tp", "seq"),
            P(),
            P("mlp", ("seq", "tp")),
            P("mlp", ("seq", "tp")),
            P(("seq", "tp"), "mlp"),
        ),
        out_specs=(P("mlp", None), P("mlp", "tp"), P("mlp", "tp")),
        check_vma=False,
    )
```

```python
import jax
import jax.numpy as jnp
from jax import lax
from jax.sharding import PartitionSpec as P

HD = 64


def rms_norm(vectors, weights):
    mean_square = jnp.mean(vectors * vectors, axis=-1, keepdims=True)
    return vectors * lax.rsqrt(mean_square + 1e-05) * weights.astype(jnp.float32)


def rotate(vectors, positions):
    half_dim = vectors.shape[-1] // 2
    inverse = 500000.0 ** (-(jnp.arange(half_dim, dtype=jnp.float32) * 2.0 / vectors.shape[-1]))
    angles = positions.astype(jnp.float32)[:, None] * inverse[None, :]
    cosine = jnp.cos(angles)[:, None, :]
    sine_part = jnp.sin(angles)[:, None, :]
    first_half = vectors[..., :half_dim]
    second_half = vectors[..., half_dim:]
    return jnp.concatenate(
        [
            first_half * cosine - second_half * sine_part,
            second_half * cosine + first_half * sine_part,
        ],
        axis=-1,
    )


def gathered_sum(x, axis):
    return jnp.sum(lax.all_gather(x, axis), axis=0)


def gather_by_exchange(x, axes):
    count = 1
    for axis in axes:
        count *= lax.axis_size(axis)
    copies = jnp.broadcast_to(x[None], (count,) + x.shape)
    return lax.all_to_all(copies, axes, 0, 0, tiled=True)


def per_device(
    hidden,
    lengths,
    attention_gain,
    query_weight,
    key_weight,
    value_weight,
    cached_keys,
    cached_values,
    output_weight,
    feedforward_gain,
    gate_weight,
    up_weight,
    down_weight,
):
    slab_rows, hidden_units = gate_weight.shape
    halves = slab_rows // hidden_units
    with jax.named_scope("mlp_weight_gather"):
        slab = jnp.concatenate(
            [gate_weight, up_weight]
            + [down_weight[:, i * hidden_units : (i + 1) * hidden_units] for i in range(halves)],
            axis=0,
        )
        blocks = lax.all_gather(slab, "mlp")
    slabs = blocks.shape[0]
    gate_full = blocks[:, :slab_rows].reshape(slabs * slab_rows, hidden_units)
    up_full = blocks[:, slab_rows : 2 * slab_rows].reshape(slabs * slab_rows, hidden_units)
    down_blocks = blocks[:, 2 * slab_rows :].reshape(slabs, halves, hidden_units, hidden_units)

    requests = hidden.shape[0]
    stream = hidden.astype(jnp.float32)
    normed = rms_norm(stream, attention_gain).astype(jnp.bfloat16)
    column_width = query_weight.shape[0]
    own_columns = lax.dynamic_slice_in_dim(
        normed, lax.axis_index("seq") * column_width, column_width, 1
    )
    query_width = query_weight.shape[1]
    key_width = key_weight.shape[1]
    with jax.named_scope("qkv_projection"):
        partial = jnp.concatenate(
            [
                jnp.dot(own_columns, query_weight, preferred_element_type=jnp.float32),
                jnp.dot(own_columns, key_weight, preferred_element_type=jnp.float32),
                jnp.dot(own_columns, value_weight, preferred_element_type=jnp.float32),
            ],
            axis=1,
        )
        total = gathered_sum(partial, "seq")
    queries_raw = total[:, :query_width]
    keys_raw = total[:, query_width : query_width + key_width]
    values_raw = total[:, query_width + key_width :]
    local_heads = query_width // HD
    key_heads = key_width // HD
    group_size = local_heads // key_heads
    queries = rotate(queries_raw.reshape(requests, local_heads, HD), lengths).astype(jnp.bfloat16)
    new_keys = (
        rotate(keys_raw.reshape(requests, key_heads, HD), lengths)
        .reshape(requests, key_heads * HD)
        .astype(jnp.bfloat16)
    )
    new_values = values_raw.astype(jnp.bfloat16)
    grouped = queries.reshape(requests, key_heads, group_size, HD)
    block_span = cached_keys.shape[1]
    key_blocks = cached_keys.reshape(requests, block_span, key_heads, HD)
    value_blocks = cached_values.reshape(requests, block_span, key_heads, HD)
    score_scale = HD ** (-0.5)
    first_position = lax.axis_index("seq") * block_span
    positions = first_position + jnp.arange(block_span, dtype=jnp.int32)
    valid_mask = (positions[None, :] < lengths[:, None])[:, None, None, :]
    with jax.named_scope("local_attention"):
        scores = (
            jnp.einsum("rgqd,rpgd->rgqp", grouped, key_blocks, preferred_element_type=jnp.float32)
            * score_scale
        )
        block_max = jnp.max(jnp.where(valid_mask, scores, -1e30), axis=-1)
        exp_weights = jnp.where(valid_mask, jnp.exp(scores - block_max[..., None]), 0.0)
        block_sum = jnp.sum(exp_weights, axis=-1)
        block_acc = jnp.einsum(
            "rgqp,rpgd->rgqd",
            exp_weights.astype(jnp.bfloat16),
            value_blocks,
            preferred_element_type=jnp.float32,
        )
    with jax.named_scope("softmax_merge"):
        state = jnp.concatenate([block_max[..., None], block_sum[..., None], block_acc], axis=-1)
        every_state = lax.all_gather(state, "seq")
        every_max = every_state[..., 0]
        every_sum = every_state[..., 1]
        every_acc = every_state[..., 2:]
        query_float = grouped.astype(jnp.float32)
        self_score = (
            jnp.sum(
                query_float * new_keys.astype(jnp.float32).reshape(requests, key_heads, 1, HD),
                axis=-1,
            )
            * score_scale
        )
        overall_max = jnp.maximum(jnp.max(every_max, axis=0), self_score)
        rescale = jnp.exp(every_max - overall_max[None])
        self_weight = jnp.exp(self_score - overall_max)
        total_weight = jnp.sum(every_sum * rescale, axis=0) + self_weight
        weighted_sum = jnp.sum(every_acc * rescale[..., None], axis=0) + self_weight[
            ..., None
        ] * new_values.astype(jnp.float32).reshape(requests, key_heads, 1, HD)
        attended = (
            (weighted_sum / total_weight[..., None])
            .reshape(requests, local_heads * HD)
            .astype(jnp.bfloat16)
        )
    with jax.named_scope("output_projection"):
        partial_output = jnp.dot(attended, output_weight, preferred_element_type=jnp.float32)
        every_partial = gather_by_exchange(partial_output.astype(jnp.bfloat16), ("seq", "tp"))
        column_blocks = lax.axis_size("seq")
        projected = (
            every_partial.reshape(column_blocks, lax.axis_size("tp"), requests, -1)
            .astype(jnp.float32)
            .sum(axis=1)
            .astype(jnp.bfloat16)
            .transpose(1, 0, 2)
            .reshape(requests, -1)
        )
    mixed_stream = stream + projected.astype(jnp.float32)
    mlp_input = rms_norm(mixed_stream, feedforward_gain).astype(jnp.bfloat16)
    with jax.named_scope("feed_forward"):
        gate = jnp.dot(mlp_input, gate_full, preferred_element_type=jnp.float32)
        upward = jnp.dot(mlp_input, up_full, preferred_element_type=jnp.float32)
        activated = (jax.nn.silu(gate) * upward).astype(jnp.bfloat16)
        down_part = jnp.einsum(
            "rh,jihc->rjic", activated, down_blocks, preferred_element_type=jnp.float32
        ).reshape(requests, slabs * slab_rows)
    with jax.named_scope("down_reduction"):
        reducers = lax.axis_size("seq") * lax.axis_size("tp")
        pieces = down_part.reshape(requests, reducers, -1).transpose(1, 0, 2)
        own_piece = lax.all_to_all(pieces, ("seq", "tp"), 0, 0, tiled=True).sum(axis=0)
        every_piece = gather_by_exchange(own_piece.astype(jnp.bfloat16), ("seq", "tp"))
        down_total = every_piece.transpose(1, 0, 2).reshape(requests, -1)
    updated_hidden = (mixed_stream + down_total.astype(jnp.float32)).astype(jnp.bfloat16)
    return (updated_hidden, new_keys, new_values)


def solution(mesh):
    return jax.shard_map(
        per_device,
        mesh=mesh,
        in_specs=(
            P("mlp", None),
            P("mlp"),
            P(),
            P("seq", "tp"),
            P("seq", "tp"),
            P("seq", "tp"),
            P("mlp", "seq", "tp"),
            P("mlp", "seq", "tp"),
            P("tp", "seq"),
            P(),
            P("mlp", ("seq", "tp")),
            P("mlp", ("seq", "tp")),
            P(("seq", "tp"), "mlp"),
        ),
        out_specs=(P("mlp", None), P("mlp", "tp"), P("mlp", "tp")),
        check_vma=False,
    )
```

```python
import jax
import jax.numpy as jnp
from jax import lax
from jax.experimental import pallas as pl
from jax.experimental.pallas import tpu as pltpu
from jax.sharding import PartitionSpec as P

HD = 64


def rms_norm(vectors, weights):
    mean_square = jnp.mean(vectors * vectors, axis=-1, keepdims=True)
    return vectors * lax.rsqrt(mean_square + 1e-05) * weights.astype(jnp.float32)


def rotate(vectors, positions):
    half_dim = vectors.shape[-1] // 2
    inverse = 500000.0 ** (-(jnp.arange(half_dim, dtype=jnp.float32) * 2.0 / vectors.shape[-1]))
    angles = positions.astype(jnp.float32)[:, None] * inverse[None, :]
    cosine = jnp.cos(angles)[:, None, :]
    sine_part = jnp.sin(angles)[:, None, :]
    first_half = vectors[..., :half_dim]
    second_half = vectors[..., half_dim:]
    return jnp.concatenate(
        [
            first_half * cosine - second_half * sine_part,
            second_half * cosine + first_half * sine_part,
        ],
        axis=-1,
    )


def projection_kernel(block_ref, hidden_ref, gain_ref, query_ref, key_ref, value_ref, out_ref):
    width = query_ref.shape[0]
    offset = pl.multiple_of(block_ref[0] * width, width)
    stream = hidden_ref[...].astype(jnp.float32)
    mean_square = jnp.mean(stream * stream, axis=-1, keepdims=True)
    columns = hidden_ref[:, pl.ds(offset, width)].astype(jnp.float32)
    gains = gain_ref[:, pl.ds(offset, width)].astype(jnp.float32)
    normed = (columns * lax.rsqrt(mean_square + 1e-05) * gains).astype(jnp.bfloat16)
    query_width = query_ref.shape[1]
    key_width = key_ref.shape[1]
    out_ref[:, :query_width] = jnp.dot(normed, query_ref[...], preferred_element_type=jnp.float32)
    out_ref[:, query_width : query_width + key_width] = jnp.dot(
        normed, key_ref[...], preferred_element_type=jnp.float32
    )
    out_ref[:, query_width + key_width :] = jnp.dot(
        normed, value_ref[...], preferred_element_type=jnp.float32
    )


def partial_projection(block, hidden, gain, query_weight, key_weight, value_weight):
    rows, features = hidden.shape
    width = query_weight.shape[0]
    total = query_weight.shape[1] + key_weight.shape[1] + value_weight.shape[1]
    vmem = pl.BlockSpec(memory_space=pltpu.VMEM)
    return pl.pallas_call(
        projection_kernel,
        out_shape=jax.ShapeDtypeStruct((rows, total), jnp.float32),
        in_specs=[pl.BlockSpec(memory_space=pltpu.SMEM)] + [vmem] * 5,
        out_specs=vmem,
        cost_estimate=pl.CostEstimate(
            flops=2 * rows * width * total,
            bytes_accessed=2 * (rows * features + features + width * total) + 4 * rows * total,
            transcendentals=rows,
        ),
    )(block, hidden, gain.reshape(1, features), query_weight, key_weight, value_weight)


def gathered_sum(x, axis):
    return jnp.sum(lax.all_gather(x, axis), axis=0)


def gather_by_exchange(x, axes):
    count = 1
    for axis in axes:
        count *= lax.axis_size(axis)
    copies = jnp.broadcast_to(x[None], (count,) + x.shape)
    return lax.all_to_all(copies, axes, 0, 0, tiled=True)


def per_device(
    hidden,
    lengths,
    attention_gain,
    query_weight,
    key_weight,
    value_weight,
    cached_keys,
    cached_values,
    output_weight,
    feedforward_gain,
    gate_weight,
    up_weight,
    down_weight,
):
    slab_rows, hidden_units = gate_weight.shape
    with jax.named_scope("mlp_weight_gather"):
        slab = jnp.concatenate(
            [jnp.concatenate([gate_weight, up_weight], axis=1), down_weight], axis=0
        )
        blocks = lax.all_gather(slab, "mlp")
    slabs = blocks.shape[0]
    gate_full = blocks[:, :slab_rows, :hidden_units].reshape(slabs * slab_rows, hidden_units)
    up_full = blocks[:, :slab_rows, hidden_units:].reshape(slabs * slab_rows, hidden_units)
    down_blocks = blocks[:, slab_rows:, :]

    requests = hidden.shape[0]
    stream = hidden.astype(jnp.float32)
    query_width = query_weight.shape[1]
    key_width = key_weight.shape[1]
    with jax.named_scope("qkv_projection"):
        block = lax.axis_index("seq").astype(jnp.int32).reshape(1)
        partial = partial_projection(
            block, hidden, attention_gain, query_weight, key_weight, value_weight
        )
        total = gathered_sum(partial, "seq")
    queries_raw = total[:, :query_width]
    keys_raw = total[:, query_width : query_width + key_width]
    values_raw = total[:, query_width + key_width :]
    local_heads = query_width // HD
    key_heads = key_width // HD
    group_size = local_heads // key_heads
    queries = rotate(queries_raw.reshape(requests, local_heads, HD), lengths).astype(jnp.bfloat16)
    new_keys = (
        rotate(keys_raw.reshape(requests, key_heads, HD), lengths)
        .reshape(requests, key_heads * HD)
        .astype(jnp.bfloat16)
    )
    new_values = values_raw.astype(jnp.bfloat16)
    grouped = queries.reshape(requests, key_heads, group_size, HD)
    block_span = cached_keys.shape[1]
    key_blocks = cached_keys.reshape(requests, block_span, key_heads, HD)
    value_blocks = cached_values.reshape(requests, block_span, key_heads, HD)
    score_scale = HD ** (-0.5)
    first_position = lax.axis_index("seq") * block_span
    positions = first_position + jnp.arange(block_span, dtype=jnp.int32)
    valid_mask = (positions[None, :] < lengths[:, None])[:, None, None, :]
    with jax.named_scope("local_attention"):
        scores = (
            jnp.einsum("rgqd,rpgd->rgqp", grouped, key_blocks, preferred_element_type=jnp.float32)
            * score_scale
        )
        block_max = jnp.max(jnp.where(valid_mask, scores, -1e30), axis=-1)
        exp_weights = jnp.where(valid_mask, jnp.exp(scores - block_max[..., None]), 0.0)
        block_sum = jnp.sum(exp_weights, axis=-1)
        block_acc = jnp.einsum(
            "rgqp,rpgd->rgqd",
            exp_weights.astype(jnp.bfloat16),
            value_blocks,
            preferred_element_type=jnp.float32,
        )
    with jax.named_scope("softmax_merge"):
        state = jnp.concatenate([block_max[..., None], block_sum[..., None], block_acc], axis=-1)
        every_state = lax.all_gather(state, "seq")
        every_max = every_state[..., 0]
        every_sum = every_state[..., 1]
        every_acc = every_state[..., 2:]
        query_float = grouped.astype(jnp.float32)
        self_score = (
            jnp.sum(
                query_float * new_keys.astype(jnp.float32).reshape(requests, key_heads, 1, HD),
                axis=-1,
            )
            * score_scale
        )
        overall_max = jnp.maximum(jnp.max(every_max, axis=0), self_score)
        rescale = jnp.exp(every_max - overall_max[None])
        self_weight = jnp.exp(self_score - overall_max)
        total_weight = jnp.sum(every_sum * rescale, axis=0) + self_weight
        weighted_sum = jnp.sum(every_acc * rescale[..., None], axis=0) + self_weight[
            ..., None
        ] * new_values.astype(jnp.float32).reshape(requests, key_heads, 1, HD)
        attended = (
            (weighted_sum / total_weight[..., None])
            .reshape(requests, local_heads * HD)
            .astype(jnp.bfloat16)
        )
    with jax.named_scope("output_projection"):
        partial_output = jnp.dot(attended, output_weight, preferred_element_type=jnp.float32)
        every_partial = gather_by_exchange(partial_output.astype(jnp.bfloat16), ("seq", "tp"))
        column_blocks = lax.axis_size("seq")
        projected = (
            every_partial.reshape(column_blocks, lax.axis_size("tp"), requests, -1)
            .astype(jnp.float32)
            .sum(axis=1)
            .astype(jnp.bfloat16)
            .transpose(1, 0, 2)
            .reshape(requests, -1)
        )
    mixed_stream = stream + projected.astype(jnp.float32)
    mlp_input = rms_norm(mixed_stream, feedforward_gain).astype(jnp.bfloat16)
    with jax.named_scope("feed_forward"):
        gate = jnp.dot(mlp_input, gate_full, preferred_element_type=jnp.float32)
        upward = jnp.dot(mlp_input, up_full, preferred_element_type=jnp.float32)
        activated = (jax.nn.silu(gate) * upward).astype(jnp.bfloat16)
        down_part = jnp.einsum(
            "rh,jhc->rjc", activated, down_blocks, preferred_element_type=jnp.float32
        ).reshape(requests, slabs * slab_rows)
    with jax.named_scope("down_reduction"):
        reducers = lax.axis_size("seq") * lax.axis_size("tp")
        pieces = down_part.reshape(requests, reducers, -1).transpose(1, 0, 2)
        own_piece = lax.all_to_all(pieces, ("seq", "tp"), 0, 0, tiled=True).sum(axis=0)
        every_piece = gather_by_exchange(own_piece.astype(jnp.bfloat16), ("seq", "tp"))
        down_total = every_piece.transpose(1, 0, 2).reshape(requests, -1)
    updated_hidden = (mixed_stream + down_total.astype(jnp.float32)).astype(jnp.bfloat16)
    return (updated_hidden, new_keys, new_values)


def solution(mesh):
    return jax.shard_map(
        per_device,
        mesh=mesh,
        in_specs=(
            P("mlp", None),
            P("mlp"),
            P(),
            P("seq", "tp"),
            P("seq", "tp"),
            P("seq", "tp"),
            P("mlp", "seq", "tp"),
            P("mlp", "seq", "tp"),
            P("tp", "seq"),
            P(),
            P("mlp", ("seq", "tp")),
            P("mlp", ("seq", "tp")),
            P(("seq", "tp"), "mlp"),
        ),
        out_specs=(P("mlp", None), P("mlp", "tp"), P("mlp", "tp")),
        check_vma=False,
    )
```

```python
import jax
import jax.numpy as jnp
from jax import lax
from jax.experimental import pallas as pl
from jax.experimental.pallas import tpu as pltpu
from jax.sharding import PartitionSpec as P

HD = 64


def rms_norm(vectors, weights):
    mean_square = jnp.mean(vectors * vectors, axis=-1, keepdims=True)
    return vectors * lax.rsqrt(mean_square + 1e-05) * weights.astype(jnp.float32)


def rotate(vectors, positions):
    half_dim = vectors.shape[-1] // 2
    inverse = 500000.0 ** (-(jnp.arange(half_dim, dtype=jnp.float32) * 2.0 / vectors.shape[-1]))
    angles = positions.astype(jnp.float32)[:, None] * inverse[None, :]
    cosine = jnp.cos(angles)[:, None, :]
    sine_part = jnp.sin(angles)[:, None, :]
    first_half = vectors[..., :half_dim]
    second_half = vectors[..., half_dim:]
    return jnp.concatenate(
        [
            first_half * cosine - second_half * sine_part,
            second_half * cosine + first_half * sine_part,
        ],
        axis=-1,
    )


def projection_kernel(
    block_ref, hidden_ref, gain_ref, query_ref, key_ref, value_ref, out_ref, normed_ref
):
    width = query_ref.shape[0]
    offset = pl.multiple_of(block_ref[0] * width, width)
    stream = hidden_ref[...].astype(jnp.float32)
    mean_square = jnp.mean(stream * stream, axis=-1, keepdims=True)
    gains = gain_ref[...].astype(jnp.float32)[None, :]
    normed_ref[...] = (stream * lax.rsqrt(mean_square + 1e-05) * gains).astype(jnp.bfloat16)
    normed = normed_ref[:, pl.ds(offset, width)]
    query_width = query_ref.shape[1]
    key_width = key_ref.shape[1]
    out_ref[:, :query_width] = jnp.dot(normed, query_ref[...], preferred_element_type=jnp.float32)
    out_ref[:, query_width : query_width + key_width] = jnp.dot(
        normed, key_ref[...], preferred_element_type=jnp.float32
    )
    out_ref[:, query_width + key_width :] = jnp.dot(
        normed, value_ref[...], preferred_element_type=jnp.float32
    )


def partial_projection(block, hidden, gain, query_weight, key_weight, value_weight):
    rows, features = hidden.shape
    width = query_weight.shape[0]
    total = query_weight.shape[1] + key_weight.shape[1] + value_weight.shape[1]
    vmem = pl.BlockSpec(memory_space=pltpu.VMEM)
    return pl.pallas_call(
        projection_kernel,
        out_shape=jax.ShapeDtypeStruct((rows, total), jnp.float32),
        in_specs=[pl.BlockSpec(memory_space=pltpu.SMEM)] + [vmem] * 5,
        out_specs=vmem,
        scratch_shapes=[pltpu.VMEM((rows, features), jnp.bfloat16)],
        cost_estimate=pl.CostEstimate(
            flops=2 * rows * width * total,
            bytes_accessed=2 * (rows * features + features + width * total) + 4 * rows * total,
            transcendentals=rows,
        ),
    )(block, hidden, gain, query_weight, key_weight, value_weight)


def gathered_sum(x, axis):
    return jnp.sum(lax.all_gather(x, axis), axis=0)


def gather_by_exchange(x, axes):
    count = 1
    for axis in axes:
        count *= lax.axis_size(axis)
    copies = jnp.broadcast_to(x[None], (count,) + x.shape)
    return lax.all_to_all(copies, axes, 0, 0, tiled=True)


def per_device(
    hidden,
    lengths,
    attention_gain,
    query_weight,
    key_weight,
    value_weight,
    cached_keys,
    cached_values,
    output_weight,
    feedforward_gain,
    gate_weight,
    up_weight,
    down_weight,
):
    slab_rows, hidden_units = gate_weight.shape
    with jax.named_scope("mlp_weight_gather"):
        slab = jnp.concatenate(
            [jnp.concatenate([gate_weight, up_weight], axis=1), down_weight], axis=0
        )
        blocks = lax.all_gather(slab, "mlp")
    slabs = blocks.shape[0]
    gate_full = blocks[:, :slab_rows, :hidden_units].reshape(slabs * slab_rows, hidden_units)
    up_full = blocks[:, :slab_rows, hidden_units:].reshape(slabs * slab_rows, hidden_units)
    down_blocks = blocks[:, slab_rows:, :]

    requests = hidden.shape[0]
    stream = hidden.astype(jnp.float32)
    query_width = query_weight.shape[1]
    key_width = key_weight.shape[1]
    with jax.named_scope("qkv_projection"):
        block = lax.axis_index("seq").astype(jnp.int32).reshape(1)
        partial = partial_projection(
            block, hidden, attention_gain, query_weight, key_weight, value_weight
        )
        total = gathered_sum(partial, "seq")
    queries_raw = total[:, :query_width]
    keys_raw = total[:, query_width : query_width + key_width]
    values_raw = total[:, query_width + key_width :]
    local_heads = query_width // HD
    key_heads = key_width // HD
    group_size = local_heads // key_heads
    queries = rotate(queries_raw.reshape(requests, local_heads, HD), lengths).astype(jnp.bfloat16)
    new_keys = (
        rotate(keys_raw.reshape(requests, key_heads, HD), lengths)
        .reshape(requests, key_heads * HD)
        .astype(jnp.bfloat16)
    )
    new_values = values_raw.astype(jnp.bfloat16)
    grouped = queries.reshape(requests, key_heads, group_size, HD)
    block_span = cached_keys.shape[1]
    key_blocks = cached_keys.reshape(requests, block_span, key_heads, HD)
    value_blocks = cached_values.reshape(requests, block_span, key_heads, HD)
    score_scale = HD ** (-0.5)
    first_position = lax.axis_index("seq") * block_span
    positions = first_position + jnp.arange(block_span, dtype=jnp.int32)
    valid_mask = (positions[None, :] < lengths[:, None])[:, None, None, :]
    with jax.named_scope("local_attention"):
        scores = (
            jnp.einsum("rgqd,rpgd->rgqp", grouped, key_blocks, preferred_element_type=jnp.float32)
            * score_scale
        )
        block_max = jnp.max(jnp.where(valid_mask, scores, -1e30), axis=-1)
        exp_weights = jnp.where(valid_mask, jnp.exp(scores - block_max[..., None]), 0.0)
        block_sum = jnp.sum(exp_weights, axis=-1)
        block_acc = jnp.einsum(
            "rgqp,rpgd->rgqd",
            exp_weights.astype(jnp.bfloat16),
            value_blocks,
            preferred_element_type=jnp.float32,
        )
    with jax.named_scope("softmax_merge"):
        state = jnp.concatenate([block_max[..., None], block_sum[..., None], block_acc], axis=-1)
        every_state = lax.all_gather(state, "seq")
        every_max = every_state[..., 0]
        every_sum = every_state[..., 1]
        every_acc = every_state[..., 2:]
        query_float = grouped.astype(jnp.float32)
        self_score = (
            jnp.sum(
                query_float * new_keys.astype(jnp.float32).reshape(requests, key_heads, 1, HD),
                axis=-1,
            )
            * score_scale
        )
        overall_max = jnp.maximum(jnp.max(every_max, axis=0), self_score)
        rescale = jnp.exp(every_max - overall_max[None])
        self_weight = jnp.exp(self_score - overall_max)
        total_weight = jnp.sum(every_sum * rescale, axis=0) + self_weight
        weighted_sum = jnp.sum(every_acc * rescale[..., None], axis=0) + self_weight[
            ..., None
        ] * new_values.astype(jnp.float32).reshape(requests, key_heads, 1, HD)
        attended = (
            (weighted_sum / total_weight[..., None])
            .reshape(requests, local_heads * HD)
            .astype(jnp.bfloat16)
        )
    with jax.named_scope("output_projection"):
        partial_output = jnp.dot(attended, output_weight, preferred_element_type=jnp.float32)
        every_partial = gather_by_exchange(partial_output.astype(jnp.bfloat16), ("seq", "tp"))
        column_blocks = lax.axis_size("seq")
        projected = (
            every_partial.reshape(column_blocks, lax.axis_size("tp"), requests, -1)
            .astype(jnp.float32)
            .sum(axis=1)
            .astype(jnp.bfloat16)
            .transpose(1, 0, 2)
            .reshape(requests, -1)
        )
    mixed_stream = stream + projected.astype(jnp.float32)
    mlp_input = rms_norm(mixed_stream, feedforward_gain).astype(jnp.bfloat16)
    with jax.named_scope("feed_forward"):
        gate = jnp.dot(mlp_input, gate_full, preferred_element_type=jnp.float32)
        upward = jnp.dot(mlp_input, up_full, preferred_element_type=jnp.float32)
        activated = (jax.nn.silu(gate) * upward).astype(jnp.bfloat16)
        down_part = jnp.einsum(
            "rh,jhc->rjc", activated, down_blocks, preferred_element_type=jnp.float32
        ).reshape(requests, slabs * slab_rows)
    with jax.named_scope("down_reduction"):
        reducers = lax.axis_size("seq") * lax.axis_size("tp")
        pieces = down_part.reshape(requests, reducers, -1).transpose(1, 0, 2)
        own_piece = lax.all_to_all(pieces, ("seq", "tp"), 0, 0, tiled=True).sum(axis=0)
        every_piece = gather_by_exchange(own_piece.astype(jnp.bfloat16), ("seq", "tp"))
        down_total = every_piece.transpose(1, 0, 2).reshape(requests, -1)
    updated_hidden = (mixed_stream + down_total.astype(jnp.float32)).astype(jnp.bfloat16)
    return (updated_hidden, new_keys, new_values)


def solution(mesh):
    return jax.shard_map(
        per_device,
        mesh=mesh,
        in_specs=(
            P("mlp", None),
            P("mlp"),
            P(),
            P("seq", "tp"),
            P("seq", "tp"),
            P("seq", "tp"),
            P("mlp", "seq", "tp"),
            P("mlp", "seq", "tp"),
            P("tp", "seq"),
            P(),
            P("mlp", ("seq", "tp")),
            P("mlp", ("seq", "tp")),
            P(("seq", "tp"), "mlp"),
        ),
        out_specs=(P("mlp", None), P("mlp", "tp"), P("mlp", "tp")),
        check_vma=False,
    )
```

```python
import jax
import jax.numpy as jnp
from jax import lax
from jax.experimental import pallas as pl
from jax.experimental.pallas import tpu as pltpu
from jax.sharding import PartitionSpec as P

HD = 64


def rms_norm(vectors, weights):
    mean_square = jnp.mean(vectors * vectors, axis=-1, keepdims=True)
    return vectors * lax.rsqrt(mean_square + 1e-05) * weights.astype(jnp.float32)


def rotate(vectors, positions):
    half_dim = vectors.shape[-1] // 2
    inverse = 500000.0 ** (-(jnp.arange(half_dim, dtype=jnp.float32) * 2.0 / vectors.shape[-1]))
    angles = positions.astype(jnp.float32)[:, None] * inverse[None, :]
    cosine = jnp.cos(angles)[:, None, :]
    sine_part = jnp.sin(angles)[:, None, :]
    first_half = vectors[..., :half_dim]
    second_half = vectors[..., half_dim:]
    return jnp.concatenate(
        [
            first_half * cosine - second_half * sine_part,
            second_half * cosine + first_half * sine_part,
        ],
        axis=-1,
    )


def projection_kernel(
    block_ref,
    hidden_ref,
    gain_ref,
    query_ref,
    key_ref,
    value_ref,
    gate_ref,
    up_ref,
    down_ref,
    out_ref,
    slab_ref,
    normed_ref,
):
    slab_rows, hidden_units = gate_ref.shape
    slab_ref[:slab_rows, :hidden_units] = gate_ref[...]
    slab_ref[:slab_rows, hidden_units:] = up_ref[...]
    slab_ref[slab_rows:, :] = down_ref[...]
    width = query_ref.shape[0]
    offset = pl.multiple_of(block_ref[0] * width, width)
    stream = hidden_ref[...].astype(jnp.float32)
    mean_square = jnp.mean(stream * stream, axis=-1, keepdims=True)
    gains = gain_ref[...].astype(jnp.float32)[None, :]
    normed_ref[...] = (stream * lax.rsqrt(mean_square + 1e-05) * gains).astype(jnp.bfloat16)
    normed = normed_ref[:, pl.ds(offset, width)]
    query_width = query_ref.shape[1]
    key_width = key_ref.shape[1]
    out_ref[:, :query_width] = jnp.dot(normed, query_ref[...], preferred_element_type=jnp.float32)
    out_ref[:, query_width : query_width + key_width] = jnp.dot(
        normed, key_ref[...], preferred_element_type=jnp.float32
    )
    out_ref[:, query_width + key_width :] = jnp.dot(
        normed, value_ref[...], preferred_element_type=jnp.float32
    )


def partial_projection(block, hidden, gain, query_weight, key_weight, value_weight, gate, up, down):
    rows, features = hidden.shape
    width = query_weight.shape[0]
    total = query_weight.shape[1] + key_weight.shape[1] + value_weight.shape[1]
    slab_shape = (gate.shape[0] + down.shape[0], gate.shape[1] + up.shape[1])
    vmem = pl.BlockSpec(memory_space=pltpu.VMEM)
    return pl.pallas_call(
        projection_kernel,
        out_shape=(
            jax.ShapeDtypeStruct((rows, total), jnp.float32),
            jax.ShapeDtypeStruct(slab_shape, gate.dtype),
        ),
        in_specs=[pl.BlockSpec(memory_space=pltpu.SMEM)] + [vmem] * 8,
        out_specs=(vmem, vmem),
        scratch_shapes=[pltpu.VMEM((rows, features), jnp.bfloat16)],
        cost_estimate=pl.CostEstimate(
            flops=2 * rows * width * total,
            bytes_accessed=2 * (rows * features + features + width * total)
            + 4 * rows * total
            + 4 * slab_shape[0] * slab_shape[1],
            transcendentals=rows,
        ),
    )(block, hidden, gain, query_weight, key_weight, value_weight, gate, up, down)


def gathered_sum(x, axis):
    return jnp.sum(lax.all_gather(x, axis), axis=0)


def gather_by_exchange(x, axes):
    count = 1
    for axis in axes:
        count *= lax.axis_size(axis)
    copies = jnp.broadcast_to(x[None], (count,) + x.shape)
    return lax.all_to_all(copies, axes, 0, 0, tiled=True)


def per_device(
    hidden,
    lengths,
    attention_gain,
    query_weight,
    key_weight,
    value_weight,
    cached_keys,
    cached_values,
    output_weight,
    feedforward_gain,
    gate_weight,
    up_weight,
    down_weight,
):
    requests = hidden.shape[0]
    stream = hidden.astype(jnp.float32)
    query_width = query_weight.shape[1]
    key_width = key_weight.shape[1]
    slab_rows, hidden_units = gate_weight.shape
    with jax.named_scope("qkv_projection"):
        block = lax.axis_index("seq").astype(jnp.int32).reshape(1)
        partial, slab = partial_projection(
            block,
            hidden,
            attention_gain,
            query_weight,
            key_weight,
            value_weight,
            gate_weight,
            up_weight,
            down_weight,
        )
    with jax.named_scope("mlp_weight_gather"):
        blocks = lax.all_gather(slab, "mlp")
    slabs = blocks.shape[0]
    gate_full = blocks[:, :slab_rows, :hidden_units].reshape(slabs * slab_rows, hidden_units)
    up_full = blocks[:, :slab_rows, hidden_units:].reshape(slabs * slab_rows, hidden_units)
    down_blocks = blocks[:, slab_rows:, :]
    with jax.named_scope("qkv_projection"):
        total = gathered_sum(partial, "seq")
    queries_raw = total[:, :query_width]
    keys_raw = total[:, query_width : query_width + key_width]
    values_raw = total[:, query_width + key_width :]
    local_heads = query_width // HD
    key_heads = key_width // HD
    group_size = local_heads // key_heads
    queries = rotate(queries_raw.reshape(requests, local_heads, HD), lengths).astype(jnp.bfloat16)
    new_keys = (
        rotate(keys_raw.reshape(requests, key_heads, HD), lengths)
        .reshape(requests, key_heads * HD)
        .astype(jnp.bfloat16)
    )
    new_values = values_raw.astype(jnp.bfloat16)
    grouped = queries.reshape(requests, key_heads, group_size, HD)
    block_span = cached_keys.shape[1]
    key_blocks = cached_keys.reshape(requests, block_span, key_heads, HD)
    value_blocks = cached_values.reshape(requests, block_span, key_heads, HD)
    score_scale = HD ** (-0.5)
    first_position = lax.axis_index("seq") * block_span
    positions = first_position + jnp.arange(block_span, dtype=jnp.int32)
    valid_mask = (positions[None, :] < lengths[:, None])[:, None, None, :]
    with jax.named_scope("local_attention"):
        scores = (
            jnp.einsum("rgqd,rpgd->rgqp", grouped, key_blocks, preferred_element_type=jnp.float32)
            * score_scale
        )
        block_max = jnp.max(jnp.where(valid_mask, scores, -1e30), axis=-1)
        exp_weights = jnp.where(valid_mask, jnp.exp(scores - block_max[..., None]), 0.0)
        block_sum = jnp.sum(exp_weights, axis=-1)
        block_acc = jnp.einsum(
            "rgqp,rpgd->rgqd",
            exp_weights.astype(jnp.bfloat16),
            value_blocks,
            preferred_element_type=jnp.float32,
        )
    with jax.named_scope("softmax_merge"):
        state = jnp.concatenate([block_max[..., None], block_sum[..., None], block_acc], axis=-1)
        every_state = lax.all_gather(state, "seq")
        every_max = every_state[..., 0]
        every_sum = every_state[..., 1]
        every_acc = every_state[..., 2:]
        query_float = grouped.astype(jnp.float32)
        self_score = (
            jnp.sum(
                query_float * new_keys.astype(jnp.float32).reshape(requests, key_heads, 1, HD),
                axis=-1,
            )
            * score_scale
        )
        overall_max = jnp.maximum(jnp.max(every_max, axis=0), self_score)
        rescale = jnp.exp(every_max - overall_max[None])
        self_weight = jnp.exp(self_score - overall_max)
        total_weight = jnp.sum(every_sum * rescale, axis=0) + self_weight
        weighted_sum = jnp.sum(every_acc * rescale[..., None], axis=0) + self_weight[
            ..., None
        ] * new_values.astype(jnp.float32).reshape(requests, key_heads, 1, HD)
        attended = (
            (weighted_sum / total_weight[..., None])
            .reshape(requests, local_heads * HD)
            .astype(jnp.bfloat16)
        )
    with jax.named_scope("output_projection"):
        partial_output = jnp.dot(attended, output_weight, preferred_element_type=jnp.float32)
        every_partial = gather_by_exchange(partial_output.astype(jnp.bfloat16), ("seq", "tp"))
        column_blocks = lax.axis_size("seq")
        projected = (
            every_partial.reshape(column_blocks, lax.axis_size("tp"), requests, -1)
            .astype(jnp.float32)
            .sum(axis=1)
            .astype(jnp.bfloat16)
            .transpose(1, 0, 2)
            .reshape(requests, -1)
        )
    mixed_stream = stream + projected.astype(jnp.float32)
    mlp_input = rms_norm(mixed_stream, feedforward_gain).astype(jnp.bfloat16)
    with jax.named_scope("feed_forward"):
        gate = jnp.dot(mlp_input, gate_full, preferred_element_type=jnp.float32)
        upward = jnp.dot(mlp_input, up_full, preferred_element_type=jnp.float32)
        activated = (jax.nn.silu(gate) * upward).astype(jnp.bfloat16)
        down_part = jnp.einsum(
            "rh,jhc->rjc", activated, down_blocks, preferred_element_type=jnp.float32
        ).reshape(requests, slabs * slab_rows)
    with jax.named_scope("down_reduction"):
        reducers = lax.axis_size("seq") * lax.axis_size("tp")
        pieces = down_part.reshape(requests, reducers, -1).transpose(1, 0, 2)
        own_piece = lax.all_to_all(pieces, ("seq", "tp"), 0, 0, tiled=True).sum(axis=0)
        every_piece = gather_by_exchange(own_piece.astype(jnp.bfloat16), ("seq", "tp"))
        down_total = every_piece.transpose(1, 0, 2).reshape(requests, -1)
    updated_hidden = (mixed_stream + down_total.astype(jnp.float32)).astype(jnp.bfloat16)
    return (updated_hidden, new_keys, new_values)


def solution(mesh):
    return jax.shard_map(
        per_device,
        mesh=mesh,
        in_specs=(
            P("mlp", None),
            P("mlp"),
            P(),
            P("seq", "tp"),
            P("seq", "tp"),
            P("seq", "tp"),
            P("mlp", "seq", "tp"),
            P("mlp", "seq", "tp"),
            P("tp", "seq"),
            P(),
            P("mlp", ("seq", "tp")),
            P("mlp", ("seq", "tp")),
            P(("seq", "tp"), "mlp"),
        ),
        out_specs=(P("mlp", None), P("mlp", "tp"), P("mlp", "tp")),
        check_vma=False,
    )
```

```python
import jax
import jax.numpy as jnp
from jax import lax
from jax.experimental import pallas as pl
from jax.experimental.pallas import tpu as pltpu
from jax.sharding import PartitionSpec as P

HD = 64


def rms_norm(vectors, weights):
    mean_square = jnp.mean(vectors * vectors, axis=-1, keepdims=True)
    return vectors * lax.rsqrt(mean_square + 1e-05) * weights.astype(jnp.float32)


def rotate(vectors, positions):
    half_dim = vectors.shape[-1] // 2
    inverse = 500000.0 ** (-(jnp.arange(half_dim, dtype=jnp.float32) * 2.0 / vectors.shape[-1]))
    angles = positions.astype(jnp.float32)[:, None] * inverse[None, :]
    cosine = jnp.cos(angles)[:, None, :]
    sine_part = jnp.sin(angles)[:, None, :]
    first_half = vectors[..., :half_dim]
    second_half = vectors[..., half_dim:]
    return jnp.concatenate(
        [
            first_half * cosine - second_half * sine_part,
            second_half * cosine + first_half * sine_part,
        ],
        axis=-1,
    )


def projection_kernel(
    block_ref,
    hidden_ref,
    gain_ref,
    query_ref,
    key_ref,
    value_ref,
    gate_ref,
    up_ref,
    down_ref,
    out_ref,
    slab_ref,
    normed_ref,
):
    slab_rows, hidden_units = gate_ref.shape
    slab_ref[:slab_rows, :hidden_units] = gate_ref[...]
    slab_ref[:slab_rows, hidden_units:] = up_ref[...]
    slab_ref[slab_rows:, :] = down_ref[...]
    width = query_ref.shape[0]
    offset = pl.multiple_of(block_ref[0] * width, width)
    stream = hidden_ref[...].astype(jnp.float32)
    mean_square = jnp.mean(stream * stream, axis=-1, keepdims=True)
    gains = gain_ref[...].astype(jnp.float32)[None, :]
    normed_ref[...] = (stream * lax.rsqrt(mean_square + 1e-05) * gains).astype(jnp.bfloat16)
    normed = normed_ref[:, pl.ds(offset, width)]
    query_width = query_ref.shape[1]
    key_width = key_ref.shape[1]
    out_ref[:, :query_width] = jnp.dot(normed, query_ref[...], preferred_element_type=jnp.float32)
    out_ref[:, query_width : query_width + key_width] = jnp.dot(
        normed, key_ref[...], preferred_element_type=jnp.float32
    )
    out_ref[:, query_width + key_width :] = jnp.dot(
        normed, value_ref[...], preferred_element_type=jnp.float32
    )


def partial_projection(block, hidden, gain, query_weight, key_weight, value_weight, gate, up, down):
    rows, features = hidden.shape
    width = query_weight.shape[0]
    total = query_weight.shape[1] + key_weight.shape[1] + value_weight.shape[1]
    slab_shape = (gate.shape[0] + down.shape[0], gate.shape[1] + up.shape[1])
    vmem = pl.BlockSpec(memory_space=pltpu.VMEM)
    return pl.pallas_call(
        projection_kernel,
        out_shape=(
            jax.ShapeDtypeStruct((rows, total), jnp.float32),
            jax.ShapeDtypeStruct(slab_shape, gate.dtype),
        ),
        in_specs=[pl.BlockSpec(memory_space=pltpu.SMEM)] + [vmem] * 8,
        out_specs=(vmem, vmem),
        scratch_shapes=[pltpu.VMEM((rows, features), jnp.bfloat16)],
        cost_estimate=pl.CostEstimate(
            flops=2 * rows * width * total,
            bytes_accessed=2 * (rows * features + features + width * total)
            + 4 * rows * total
            + 4 * slab_shape[0] * slab_shape[1],
            transcendentals=rows,
        ),
    )(block, hidden, gain, query_weight, key_weight, value_weight, gate, up, down)


def feed_forward_kernel(input_ref, blocks_ref, out_ref):
    slabs = blocks_ref.shape[0]
    slab_rows = blocks_ref.shape[1] - blocks_ref.shape[2] // 2
    hidden_units = blocks_ref.shape[2] // 2
    gate = None
    upward = None
    for j in range(slabs):
        rows = input_ref[:, j * slab_rows : (j + 1) * slab_rows]
        gate_part = jnp.dot(
            rows, blocks_ref[j, :slab_rows, :hidden_units], preferred_element_type=jnp.float32
        )
        up_part = jnp.dot(
            rows, blocks_ref[j, :slab_rows, hidden_units:], preferred_element_type=jnp.float32
        )
        gate = gate_part if gate is None else gate + gate_part
        upward = up_part if upward is None else upward + up_part
    activated = (jax.nn.silu(gate) * upward).astype(jnp.bfloat16)
    for j in range(slabs):
        out_ref[:, j * slab_rows : (j + 1) * slab_rows] = jnp.dot(
            activated, blocks_ref[j, slab_rows:, :], preferred_element_type=jnp.float32
        )


def feed_forward(mlp_input, blocks):
    rows, features = mlp_input.shape
    slabs, slab_height, slab_width = blocks.shape
    vmem = pl.BlockSpec(memory_space=pltpu.VMEM)
    return pl.pallas_call(
        feed_forward_kernel,
        out_shape=jax.ShapeDtypeStruct((rows, features), jnp.float32),
        in_specs=[vmem, vmem],
        out_specs=vmem,
        cost_estimate=pl.CostEstimate(
            flops=2 * rows * slabs * slab_height * slab_width,
            bytes_accessed=2 * rows * features + 2 * slabs * slab_height * slab_width + 4 * rows * features,
            transcendentals=rows * slab_width // 2,
        ),
    )(mlp_input, blocks)


def gathered_sum(x, axis):
    return jnp.sum(lax.all_gather(x, axis), axis=0)


def gather_by_exchange(x, axes):
    count = 1
    for axis in axes:
        count *= lax.axis_size(axis)
    copies = jnp.broadcast_to(x[None], (count,) + x.shape)
    return lax.all_to_all(copies, axes, 0, 0, tiled=True)


def per_device(
    hidden,
    lengths,
    attention_gain,
    query_weight,
    key_weight,
    value_weight,
    cached_keys,
    cached_values,
    output_weight,
    feedforward_gain,
    gate_weight,
    up_weight,
    down_weight,
):
    requests = hidden.shape[0]
    stream = hidden.astype(jnp.float32)
    query_width = query_weight.shape[1]
    key_width = key_weight.shape[1]
    slab_rows, hidden_units = gate_weight.shape
    with jax.named_scope("qkv_projection"):
        block = lax.axis_index("seq").astype(jnp.int32).reshape(1)
        partial, slab = partial_projection(
            block,
            hidden,
            attention_gain,
            query_weight,
            key_weight,
            value_weight,
            gate_weight,
            up_weight,
            down_weight,
        )
    with jax.named_scope("mlp_weight_gather"):
        blocks = lax.all_gather(slab, "mlp")
    with jax.named_scope("qkv_projection"):
        total = gathered_sum(partial, "seq")
    queries_raw = total[:, :query_width]
    keys_raw = total[:, query_width : query_width + key_width]
    values_raw = total[:, query_width + key_width :]
    local_heads = query_width // HD
    key_heads = key_width // HD
    group_size = local_heads // key_heads
    queries = rotate(queries_raw.reshape(requests, local_heads, HD), lengths).astype(jnp.bfloat16)
    new_keys = (
        rotate(keys_raw.reshape(requests, key_heads, HD), lengths)
        .reshape(requests, key_heads * HD)
        .astype(jnp.bfloat16)
    )
    new_values = values_raw.astype(jnp.bfloat16)
    grouped = queries.reshape(requests, key_heads, group_size, HD)
    block_span = cached_keys.shape[1]
    key_blocks = cached_keys.reshape(requests, block_span, key_heads, HD)
    value_blocks = cached_values.reshape(requests, block_span, key_heads, HD)
    score_scale = HD ** (-0.5)
    first_position = lax.axis_index("seq") * block_span
    positions = first_position + jnp.arange(block_span, dtype=jnp.int32)
    valid_mask = (positions[None, :] < lengths[:, None])[:, None, None, :]
    with jax.named_scope("local_attention"):
        scores = (
            jnp.einsum("rgqd,rpgd->rgqp", grouped, key_blocks, preferred_element_type=jnp.float32)
            * score_scale
        )
        block_max = jnp.max(jnp.where(valid_mask, scores, -1e30), axis=-1)
        exp_weights = jnp.where(valid_mask, jnp.exp(scores - block_max[..., None]), 0.0)
        block_sum = jnp.sum(exp_weights, axis=-1)
        block_acc = jnp.einsum(
            "rgqp,rpgd->rgqd",
            exp_weights.astype(jnp.bfloat16),
            value_blocks,
            preferred_element_type=jnp.float32,
        )
    with jax.named_scope("softmax_merge"):
        state = jnp.concatenate([block_max[..., None], block_sum[..., None], block_acc], axis=-1)
        every_state = lax.all_gather(state, "seq")
        every_max = every_state[..., 0]
        every_sum = every_state[..., 1]
        every_acc = every_state[..., 2:]
        query_float = grouped.astype(jnp.float32)
        self_score = (
            jnp.sum(
                query_float * new_keys.astype(jnp.float32).reshape(requests, key_heads, 1, HD),
                axis=-1,
            )
            * score_scale
        )
        overall_max = jnp.maximum(jnp.max(every_max, axis=0), self_score)
        rescale = jnp.exp(every_max - overall_max[None])
        self_weight = jnp.exp(self_score - overall_max)
        total_weight = jnp.sum(every_sum * rescale, axis=0) + self_weight
        weighted_sum = jnp.sum(every_acc * rescale[..., None], axis=0) + self_weight[
            ..., None
        ] * new_values.astype(jnp.float32).reshape(requests, key_heads, 1, HD)
        attended = (
            (weighted_sum / total_weight[..., None])
            .reshape(requests, local_heads * HD)
            .astype(jnp.bfloat16)
        )
    with jax.named_scope("output_projection"):
        partial_output = jnp.dot(attended, output_weight, preferred_element_type=jnp.float32)
        every_partial = gather_by_exchange(partial_output.astype(jnp.bfloat16), ("seq", "tp"))
        column_blocks = lax.axis_size("seq")
        projected = (
            every_partial.reshape(column_blocks, lax.axis_size("tp"), requests, -1)
            .astype(jnp.float32)
            .sum(axis=1)
            .astype(jnp.bfloat16)
            .transpose(1, 0, 2)
            .reshape(requests, -1)
        )
    mixed_stream = stream + projected.astype(jnp.float32)
    mlp_input = rms_norm(mixed_stream, feedforward_gain).astype(jnp.bfloat16)
    with jax.named_scope("feed_forward"):
        down_part = feed_forward(mlp_input, blocks)
    with jax.named_scope("down_reduction"):
        reducers = lax.axis_size("seq") * lax.axis_size("tp")
        pieces = down_part.reshape(requests, reducers, -1).transpose(1, 0, 2)
        own_piece = lax.all_to_all(pieces, ("seq", "tp"), 0, 0, tiled=True).sum(axis=0)
        every_piece = gather_by_exchange(own_piece.astype(jnp.bfloat16), ("seq", "tp"))
        down_total = every_piece.transpose(1, 0, 2).reshape(requests, -1)
    updated_hidden = (mixed_stream + down_total.astype(jnp.float32)).astype(jnp.bfloat16)
    return (updated_hidden, new_keys, new_values)


def solution(mesh):
    return jax.shard_map(
        per_device,
        mesh=mesh,
        in_specs=(
            P("mlp", None),
            P("mlp"),
            P(),
            P("seq", "tp"),
            P("seq", "tp"),
            P("seq", "tp"),
            P("mlp", "seq", "tp"),
            P("mlp", "seq", "tp"),
            P("tp", "seq"),
            P(),
            P("mlp", ("seq", "tp")),
            P("mlp", ("seq", "tp")),
            P(("seq", "tp"), "mlp"),
        ),
        out_specs=(P("mlp", None), P("mlp", "tp"), P("mlp", "tp")),
        check_vma=False,
    )
```

```python
import jax
import jax.numpy as jnp
from jax import lax
from jax.experimental import pallas as pl
from jax.experimental.pallas import tpu as pltpu
from jax.sharding import PartitionSpec as P

HD = 64


def rms_norm(vectors, weights):
    mean_square = jnp.mean(vectors * vectors, axis=-1, keepdims=True)
    return vectors * lax.rsqrt(mean_square + 1e-05) * weights.astype(jnp.float32)


def rotate(vectors, positions):
    half_dim = vectors.shape[-1] // 2
    inverse = 500000.0 ** (-(jnp.arange(half_dim, dtype=jnp.float32) * 2.0 / vectors.shape[-1]))
    angles = positions.astype(jnp.float32)[:, None] * inverse[None, :]
    cosine = jnp.cos(angles)[:, None, :]
    sine_part = jnp.sin(angles)[:, None, :]
    first_half = vectors[..., :half_dim]
    second_half = vectors[..., half_dim:]
    return jnp.concatenate(
        [
            first_half * cosine - second_half * sine_part,
            second_half * cosine + first_half * sine_part,
        ],
        axis=-1,
    )


def projection_kernel(
    block_ref,
    hidden_ref,
    gain_ref,
    query_ref,
    key_ref,
    value_ref,
    gate_ref,
    up_ref,
    down_ref,
    out_ref,
    slab_ref,
    normed_ref,
):
    slab_rows, hidden_units = gate_ref.shape
    slab_ref[:slab_rows, :hidden_units] = gate_ref[...]
    slab_ref[:slab_rows, hidden_units:] = up_ref[...]
    slab_ref[slab_rows:, :] = down_ref[...]
    width = query_ref.shape[0]
    offset = pl.multiple_of(block_ref[0] * width, width)
    stream = hidden_ref[...].astype(jnp.float32)
    mean_square = jnp.mean(stream * stream, axis=-1, keepdims=True)
    gains = gain_ref[...].astype(jnp.float32)[None, :]
    normed_ref[...] = (stream * lax.rsqrt(mean_square + 1e-05) * gains).astype(jnp.bfloat16)
    normed = normed_ref[:, pl.ds(offset, width)]
    query_width = query_ref.shape[1]
    key_width = key_ref.shape[1]
    out_ref[:, :query_width] = jnp.dot(normed, query_ref[...], preferred_element_type=jnp.float32)
    out_ref[:, query_width : query_width + key_width] = jnp.dot(
        normed, key_ref[...], preferred_element_type=jnp.float32
    )
    out_ref[:, query_width + key_width :] = jnp.dot(
        normed, value_ref[...], preferred_element_type=jnp.float32
    )


def partial_projection(block, hidden, gain, query_weight, key_weight, value_weight, gate, up, down):
    rows, features = hidden.shape
    width = query_weight.shape[0]
    total = query_weight.shape[1] + key_weight.shape[1] + value_weight.shape[1]
    slab_shape = (gate.shape[0] + down.shape[0], gate.shape[1] + up.shape[1])
    vmem = pl.BlockSpec(memory_space=pltpu.VMEM)
    return pl.pallas_call(
        projection_kernel,
        out_shape=(
            jax.ShapeDtypeStruct((rows, total), jnp.float32),
            jax.ShapeDtypeStruct(slab_shape, gate.dtype),
        ),
        in_specs=[pl.BlockSpec(memory_space=pltpu.SMEM)] + [vmem] * 8,
        out_specs=(vmem, vmem),
        scratch_shapes=[pltpu.VMEM((rows, features), jnp.bfloat16)],
        cost_estimate=pl.CostEstimate(
            flops=2 * rows * width * total,
            bytes_accessed=2 * (rows * features + features + width * total)
            + 4 * rows * total
            + 4 * slab_shape[0] * slab_shape[1],
            transcendentals=rows,
        ),
    )(block, hidden, gain, query_weight, key_weight, value_weight, gate, up, down)


def combine_kernel(state_ref, self_ref, values_ref, weight_ref, out_ref):
    head_dim = values_ref.shape[-1]
    state = state_ref[...]
    block_max = state[..., head_dim : head_dim + 1]
    block_sum = state[..., head_dim + 1 : head_dim + 2]
    block_acc = state[..., :head_dim]
    self_score = self_ref[...]
    overall_max = jnp.maximum(jnp.max(block_max, axis=0), self_score)
    rescale = jnp.exp(block_max - overall_max[None])
    self_weight = jnp.exp(self_score - overall_max)
    total_weight = jnp.sum(block_sum * rescale, axis=0) + self_weight
    weighted_sum = jnp.sum(block_acc * rescale, axis=0) + self_weight * values_ref[...]
    attended = (weighted_sum / total_weight).astype(jnp.bfloat16)
    projected = None
    for head in range(attended.shape[0]):
        term = jnp.dot(
            attended[head],
            weight_ref[head * head_dim : (head + 1) * head_dim, :],
            preferred_element_type=jnp.float32,
        )
        projected = term if projected is None else projected + term
    out_ref[...] = jnp.broadcast_to(projected.astype(out_ref.dtype)[None], out_ref.shape)


def combine_and_project(every_state, self_score, head_values, output_weight, copies):
    blocks, heads, rows, lanes = every_state.shape
    width = output_weight.shape[1]
    vmem = pl.BlockSpec(memory_space=pltpu.VMEM)
    return pl.pallas_call(
        combine_kernel,
        out_shape=jax.ShapeDtypeStruct((copies, rows, width), jnp.bfloat16),
        in_specs=[vmem] * 4,
        out_specs=vmem,
        cost_estimate=pl.CostEstimate(
            flops=2 * rows * output_weight.shape[0] * width + 4 * blocks * heads * rows * lanes,
            bytes_accessed=4 * blocks * heads * rows * lanes
            + 2 * output_weight.size
            + 2 * copies * rows * width,
            transcendentals=blocks * heads * rows,
        ),
    )(every_state, self_score, head_values, output_weight)


def gathered_sum(x, axis):
    return jnp.sum(lax.all_gather(x, axis), axis=0)


def gather_by_exchange(x, axes):
    count = 1
    for axis in axes:
        count *= lax.axis_size(axis)
    copies = jnp.broadcast_to(x[None], (count,) + x.shape)
    return lax.all_to_all(copies, axes, 0, 0, tiled=True)


def per_device(
    hidden,
    lengths,
    attention_gain,
    query_weight,
    key_weight,
    value_weight,
    cached_keys,
    cached_values,
    output_weight,
    feedforward_gain,
    gate_weight,
    up_weight,
    down_weight,
):
    requests = hidden.shape[0]
    stream = hidden.astype(jnp.float32)
    query_width = query_weight.shape[1]
    key_width = key_weight.shape[1]
    slab_rows, hidden_units = gate_weight.shape
    with jax.named_scope("qkv_projection"):
        block = lax.axis_index("seq").astype(jnp.int32).reshape(1)
        partial, slab = partial_projection(
            block,
            hidden,
            attention_gain,
            query_weight,
            key_weight,
            value_weight,
            gate_weight,
            up_weight,
            down_weight,
        )
    with jax.named_scope("mlp_weight_gather"):
        blocks = lax.all_gather(slab, "mlp")
    slabs = blocks.shape[0]
    gate_full = blocks[:, :slab_rows, :hidden_units].reshape(slabs * slab_rows, hidden_units)
    up_full = blocks[:, :slab_rows, hidden_units:].reshape(slabs * slab_rows, hidden_units)
    down_blocks = blocks[:, slab_rows:, :]
    with jax.named_scope("qkv_projection"):
        total = gathered_sum(partial, "seq")
    queries_raw = total[:, :query_width]
    keys_raw = total[:, query_width : query_width + key_width]
    values_raw = total[:, query_width + key_width :]
    local_heads = query_width // HD
    key_heads = key_width // HD
    group_size = local_heads // key_heads
    queries = rotate(queries_raw.reshape(requests, local_heads, HD), lengths).astype(jnp.bfloat16)
    new_keys = (
        rotate(keys_raw.reshape(requests, key_heads, HD), lengths)
        .reshape(requests, key_heads * HD)
        .astype(jnp.bfloat16)
    )
    new_values = values_raw.astype(jnp.bfloat16)
    grouped = queries.reshape(requests, key_heads, group_size, HD)
    block_span = cached_keys.shape[1]
    key_blocks = cached_keys.reshape(requests, block_span, key_heads, HD)
    value_blocks = cached_values.reshape(requests, block_span, key_heads, HD)
    score_scale = HD ** (-0.5)
    first_position = lax.axis_index("seq") * block_span
    positions = first_position + jnp.arange(block_span, dtype=jnp.int32)
    valid_mask = (positions[None, :] < lengths[:, None])[:, None, None, :]
    with jax.named_scope("local_attention"):
        scores = (
            jnp.einsum("rgqd,rpgd->rgqp", grouped, key_blocks, preferred_element_type=jnp.float32)
            * score_scale
        )
        block_max = jnp.max(jnp.where(valid_mask, scores, -1e30), axis=-1)
        exp_weights = jnp.where(valid_mask, jnp.exp(scores - block_max[..., None]), 0.0)
        block_sum = jnp.sum(exp_weights, axis=-1)
        block_acc = jnp.einsum(
            "rgqp,rpgd->rgqd",
            exp_weights.astype(jnp.bfloat16),
            value_blocks,
            preferred_element_type=jnp.float32,
        )
    with jax.named_scope("softmax_merge"):
        lanes = 2 * HD
        state = jnp.concatenate(
            [
                block_acc.transpose(1, 2, 0, 3).reshape(local_heads, requests, HD),
                block_max.transpose(1, 2, 0).reshape(local_heads, requests, 1),
                block_sum.transpose(1, 2, 0).reshape(local_heads, requests, 1),
                jnp.zeros((local_heads, requests, lanes - HD - 2), jnp.float32),
            ],
            axis=-1,
        )
        every_state = lax.all_gather(state, "seq")
        query_float = grouped.astype(jnp.float32)
        self_score = (
            jnp.sum(
                query_float * new_keys.astype(jnp.float32).reshape(requests, key_heads, 1, HD),
                axis=-1,
            )
            * score_scale
        )
        self_score = self_score.transpose(1, 2, 0).reshape(local_heads, requests, 1)
        head_values = jnp.broadcast_to(
            new_values.astype(jnp.float32).reshape(requests, key_heads, 1, HD),
            (requests, key_heads, group_size, HD),
        ).transpose(1, 2, 0, 3).reshape(local_heads, requests, HD)
    with jax.named_scope("output_projection"):
        copies = lax.axis_size("seq") * lax.axis_size("tp")
        every_partial = lax.all_to_all(
            combine_and_project(every_state, self_score, head_values, output_weight, copies),
            ("seq", "tp"),
            0,
            0,
            tiled=True,
        )
        column_blocks = lax.axis_size("seq")
        projected = (
            every_partial.reshape(column_blocks, lax.axis_size("tp"), requests, -1)
            .astype(jnp.float32)
            .sum(axis=1)
            .astype(jnp.bfloat16)
            .transpose(1, 0, 2)
            .reshape(requests, -1)
        )
    mixed_stream = stream + projected.astype(jnp.float32)
    mlp_input = rms_norm(mixed_stream, feedforward_gain).astype(jnp.bfloat16)
    with jax.named_scope("feed_forward"):
        gate = jnp.dot(mlp_input, gate_full, preferred_element_type=jnp.float32)
        upward = jnp.dot(mlp_input, up_full, preferred_element_type=jnp.float32)
        activated = (jax.nn.silu(gate) * upward).astype(jnp.bfloat16)
        down_part = jnp.einsum(
            "rh,jhc->rjc", activated, down_blocks, preferred_element_type=jnp.float32
        ).reshape(requests, slabs * slab_rows)
    with jax.named_scope("down_reduction"):
        reducers = lax.axis_size("seq") * lax.axis_size("tp")
        pieces = down_part.reshape(requests, reducers, -1).transpose(1, 0, 2)
        own_piece = lax.all_to_all(pieces, ("seq", "tp"), 0, 0, tiled=True).sum(axis=0)
        every_piece = gather_by_exchange(own_piece.astype(jnp.bfloat16), ("seq", "tp"))
        down_total = every_piece.transpose(1, 0, 2).reshape(requests, -1)
    updated_hidden = (mixed_stream + down_total.astype(jnp.float32)).astype(jnp.bfloat16)
    return (updated_hidden, new_keys, new_values)


def solution(mesh):
    return jax.shard_map(
        per_device,
        mesh=mesh,
        in_specs=(
            P("mlp", None),
            P("mlp"),
            P(),
            P("seq", "tp"),
            P("seq", "tp"),
            P("seq", "tp"),
            P("mlp", "seq", "tp"),
            P("mlp", "seq", "tp"),
            P("tp", "seq"),
            P(),
            P("mlp", ("seq", "tp")),
            P("mlp", ("seq", "tp")),
            P(("seq", "tp"), "mlp"),
        ),
        out_specs=(P("mlp", None), P("mlp", "tp"), P("mlp", "tp")),
        check_vma=False,
    )
```

```python
import jax
import jax.numpy as jnp
from jax import lax
from jax.experimental import pallas as pl
from jax.experimental.pallas import tpu as pltpu
from jax.sharding import PartitionSpec as P

HD = 64


def rms_norm(vectors, weights):
    mean_square = jnp.mean(vectors * vectors, axis=-1, keepdims=True)
    return vectors * lax.rsqrt(mean_square + 1e-05) * weights.astype(jnp.float32)


def rotate(vectors, positions):
    half_dim = vectors.shape[-1] // 2
    inverse = 500000.0 ** (-(jnp.arange(half_dim, dtype=jnp.float32) * 2.0 / vectors.shape[-1]))
    angles = positions.astype(jnp.float32)[:, None] * inverse[None, :]
    cosine = jnp.cos(angles)[:, None, :]
    sine_part = jnp.sin(angles)[:, None, :]
    first_half = vectors[..., :half_dim]
    second_half = vectors[..., half_dim:]
    return jnp.concatenate(
        [
            first_half * cosine - second_half * sine_part,
            second_half * cosine + first_half * sine_part,
        ],
        axis=-1,
    )


def projection_kernel(
    block_ref,
    hidden_ref,
    gain_ref,
    query_ref,
    key_ref,
    value_ref,
    gate_ref,
    up_ref,
    down_ref,
    out_ref,
    slab_ref,
    normed_ref,
):
    slab_rows, hidden_units = gate_ref.shape
    slab_ref[:slab_rows, :hidden_units] = gate_ref[...]
    slab_ref[:slab_rows, hidden_units:] = up_ref[...]
    slab_ref[slab_rows:, :] = down_ref[...]
    width = query_ref.shape[0]
    offset = pl.multiple_of(block_ref[0] * width, width)
    stream = hidden_ref[...].astype(jnp.float32)
    mean_square = jnp.mean(stream * stream, axis=-1, keepdims=True)
    gains = gain_ref[...].astype(jnp.float32)[None, :]
    normed_ref[...] = (stream * lax.rsqrt(mean_square + 1e-05) * gains).astype(jnp.bfloat16)
    normed = normed_ref[:, pl.ds(offset, width)]
    query_width = query_ref.shape[1]
    key_width = key_ref.shape[1]
    out_ref[:, :query_width] = jnp.dot(normed, query_ref[...], preferred_element_type=jnp.float32)
    out_ref[:, query_width : query_width + key_width] = jnp.dot(
        normed, key_ref[...], preferred_element_type=jnp.float32
    )
    out_ref[:, query_width + key_width :] = jnp.dot(
        normed, value_ref[...], preferred_element_type=jnp.float32
    )


def partial_projection(block, hidden, gain, query_weight, key_weight, value_weight, gate, up, down):
    rows, features = hidden.shape
    width = query_weight.shape[0]
    total = query_weight.shape[1] + key_weight.shape[1] + value_weight.shape[1]
    slab_shape = (gate.shape[0] + down.shape[0], gate.shape[1] + up.shape[1])
    vmem = pl.BlockSpec(memory_space=pltpu.VMEM)
    return pl.pallas_call(
        projection_kernel,
        out_shape=(
            jax.ShapeDtypeStruct((rows, total), jnp.float32),
            jax.ShapeDtypeStruct(slab_shape, gate.dtype),
        ),
        in_specs=[pl.BlockSpec(memory_space=pltpu.SMEM)] + [vmem] * 8,
        out_specs=(vmem, vmem),
        scratch_shapes=[pltpu.VMEM((rows, features), jnp.bfloat16)],
        cost_estimate=pl.CostEstimate(
            flops=2 * rows * width * total,
            bytes_accessed=2 * (rows * features + features + width * total)
            + 4 * rows * total
            + 4 * slab_shape[0] * slab_shape[1],
            transcendentals=rows,
        ),
    )(block, hidden, gain, query_weight, key_weight, value_weight, gate, up, down)


def gathered_sum(x, axis):
    return jnp.sum(lax.all_gather(x, axis), axis=0)


def gather_by_exchange(x, axes):
    count = 1
    for axis in axes:
        count *= lax.axis_size(axis)
    copies = jnp.broadcast_to(x[None], (count,) + x.shape)
    return lax.all_to_all(copies, axes, 0, 0, tiled=True)


def per_device(
    hidden,
    lengths,
    attention_gain,
    query_weight,
    key_weight,
    value_weight,
    cached_keys,
    cached_values,
    output_weight,
    feedforward_gain,
    gate_weight,
    up_weight,
    down_weight,
):
    requests = hidden.shape[0]
    stream = hidden.astype(jnp.float32)
    query_width = query_weight.shape[1]
    key_width = key_weight.shape[1]
    slab_rows, hidden_units = gate_weight.shape
    with jax.named_scope("qkv_projection"):
        block = lax.axis_index("seq").astype(jnp.int32).reshape(1)
        partial, slab = partial_projection(
            block,
            hidden,
            attention_gain,
            query_weight,
            key_weight,
            value_weight,
            gate_weight,
            up_weight,
            down_weight,
        )
    with jax.named_scope("mlp_weight_gather"):
        blocks = lax.all_gather(slab, "mlp")
    slabs = blocks.shape[0]
    gate_full = blocks[:, :slab_rows, :hidden_units].reshape(slabs * slab_rows, hidden_units)
    up_full = blocks[:, :slab_rows, hidden_units:].reshape(slabs * slab_rows, hidden_units)
    down_blocks = blocks[:, slab_rows:, :]
    with jax.named_scope("qkv_projection"):
        total = gathered_sum(partial, "seq")
    queries_raw = total[:, :query_width]
    keys_raw = total[:, query_width : query_width + key_width]
    values_raw = total[:, query_width + key_width :]
    local_heads = query_width // HD
    key_heads = key_width // HD
    group_size = local_heads // key_heads
    queries = rotate(queries_raw.reshape(requests, local_heads, HD), lengths).astype(jnp.bfloat16)
    new_keys = (
        rotate(keys_raw.reshape(requests, key_heads, HD), lengths)
        .reshape(requests, key_heads * HD)
        .astype(jnp.bfloat16)
    )
    new_values = values_raw.astype(jnp.bfloat16)
    grouped = queries.reshape(requests, key_heads, group_size, HD)
    block_span = cached_keys.shape[1]
    key_blocks = cached_keys.reshape(requests, block_span, key_heads, HD)
    value_blocks = cached_values.reshape(requests, block_span, key_heads, HD)
    score_scale = HD ** (-0.5)
    first_position = lax.axis_index("seq") * block_span
    positions = first_position + jnp.arange(block_span, dtype=jnp.int32)
    valid_mask = (positions[None, :] < lengths[:, None])[:, None, None, :]
    with jax.named_scope("local_attention"):
        scores = (
            jnp.einsum("rgqd,rpgd->rgqp", grouped, key_blocks, preferred_element_type=jnp.float32)
            * score_scale
        )
        block_max = jnp.max(jnp.where(valid_mask, scores, -1e30), axis=-1)
        exp_weights = jnp.where(valid_mask, jnp.exp(scores - block_max[..., None]), 0.0)
        block_sum = jnp.sum(exp_weights, axis=-1)
        block_acc = jnp.einsum(
            "rgqp,rpgd->rgqd",
            exp_weights.astype(jnp.bfloat16),
            value_blocks,
            preferred_element_type=jnp.float32,
        )
    with jax.named_scope("softmax_merge"):
        state = jnp.concatenate([block_max[..., None], block_sum[..., None], block_acc], axis=-1)
        every_state = lax.all_gather(state, "seq")
        every_max = every_state[..., 0]
        every_sum = every_state[..., 1]
        every_acc = every_state[..., 2:]
        query_float = grouped.astype(jnp.float32)
        self_score = (
            jnp.sum(
                query_float * new_keys.astype(jnp.float32).reshape(requests, key_heads, 1, HD),
                axis=-1,
            )
            * score_scale
        )
        overall_max = jnp.maximum(jnp.max(every_max, axis=0), self_score)
        rescale = jnp.exp(every_max - overall_max[None])
        self_weight = jnp.exp(self_score - overall_max)
        total_weight = jnp.sum(every_sum * rescale, axis=0) + self_weight
        weighted_sum = jnp.sum(every_acc * rescale[..., None], axis=0) + self_weight[
            ..., None
        ] * new_values.astype(jnp.float32).reshape(requests, key_heads, 1, HD)
        attended = (
            (weighted_sum / total_weight[..., None])
            .reshape(requests, local_heads * HD)
            .astype(jnp.bfloat16)
        )
    with jax.named_scope("output_projection"):
        partial_output = jnp.dot(attended, output_weight, preferred_element_type=jnp.float32)
        every_partial = gather_by_exchange(partial_output.astype(jnp.bfloat16), ("seq", "tp"))
        column_blocks = lax.axis_size("seq")
        projected = (
            every_partial.reshape(column_blocks, lax.axis_size("tp"), requests, -1)
            .astype(jnp.float32)
            .sum(axis=1)
            .astype(jnp.bfloat16)
            .transpose(1, 0, 2)
            .reshape(requests, -1)
        )
    mixed_stream = stream + projected.astype(jnp.float32)
    mlp_input = rms_norm(mixed_stream, feedforward_gain).astype(jnp.bfloat16)
    with jax.named_scope("feed_forward"):
        gate = jnp.dot(mlp_input, gate_full, preferred_element_type=jnp.float32)
        upward = jnp.dot(mlp_input, up_full, preferred_element_type=jnp.float32)
        activated = (jax.nn.silu(gate) * upward).astype(jnp.bfloat16)
        down_part = jnp.einsum(
            "rh,jhc->rjc", activated, down_blocks, preferred_element_type=jnp.float32
        ).reshape(requests, slabs * slab_rows)
    with jax.named_scope("down_reduction"):
        reducers = lax.axis_size("seq") * lax.axis_size("tp")
        pieces = down_part.reshape(requests, reducers, -1).transpose(1, 0, 2)
        own_piece = (
            lax.all_to_all(pieces.astype(jnp.bfloat16), ("seq", "tp"), 0, 0, tiled=True)
            .astype(jnp.float32)
            .sum(axis=0)
        )
        every_piece = gather_by_exchange(own_piece.astype(jnp.bfloat16), ("seq", "tp"))
        down_total = every_piece.transpose(1, 0, 2).reshape(requests, -1)
    updated_hidden = (mixed_stream + down_total.astype(jnp.float32)).astype(jnp.bfloat16)
    return (updated_hidden, new_keys, new_values)


def solution(mesh):
    return jax.shard_map(
        per_device,
        mesh=mesh,
        in_specs=(
            P("mlp", None),
            P("mlp"),
            P(),
            P("seq", "tp"),
            P("seq", "tp"),
            P("seq", "tp"),
            P("mlp", "seq", "tp"),
            P("mlp", "seq", "tp"),
            P("tp", "seq"),
            P(),
            P("mlp", ("seq", "tp")),
            P("mlp", ("seq", "tp")),
            P(("seq", "tp"), "mlp"),
        ),
        out_specs=(P("mlp", None), P("mlp", "tp"), P("mlp", "tp")),
        check_vma=False,
    )
```

```python
import jax
import jax.numpy as jnp
from jax import lax
from jax.experimental import pallas as pl
from jax.experimental.pallas import tpu as pltpu
from jax.sharding import PartitionSpec as P

HD = 64


def rms_norm(vectors, weights):
    mean_square = jnp.mean(vectors * vectors, axis=-1, keepdims=True)
    return vectors * lax.rsqrt(mean_square + 1e-05) * weights.astype(jnp.float32)


def rotate(vectors, positions):
    half_dim = vectors.shape[-1] // 2
    inverse = 500000.0 ** (-(jnp.arange(half_dim, dtype=jnp.float32) * 2.0 / vectors.shape[-1]))
    angles = positions.astype(jnp.float32)[:, None] * inverse[None, :]
    cosine = jnp.cos(angles)[:, None, :]
    sine_part = jnp.sin(angles)[:, None, :]
    first_half = vectors[..., :half_dim]
    second_half = vectors[..., half_dim:]
    return jnp.concatenate(
        [
            first_half * cosine - second_half * sine_part,
            second_half * cosine + first_half * sine_part,
        ],
        axis=-1,
    )


def projection_kernel(
    block_ref,
    hidden_ref,
    gain_ref,
    query_ref,
    key_ref,
    value_ref,
    gate_ref,
    up_ref,
    down_ref,
    out_ref,
    slab_ref,
    normed_ref,
):
    slab_rows, hidden_units = gate_ref.shape
    slab_ref[:slab_rows, :hidden_units] = gate_ref[...]
    slab_ref[:slab_rows, hidden_units:] = up_ref[...]
    slab_ref[slab_rows:, :] = down_ref[...]
    width = query_ref.shape[0]
    offset = pl.multiple_of(block_ref[0] * width, width)
    stream = hidden_ref[...].astype(jnp.float32)
    mean_square = jnp.mean(stream * stream, axis=-1, keepdims=True)
    gains = gain_ref[...].astype(jnp.float32)[None, :]
    normed_ref[...] = (stream * lax.rsqrt(mean_square + 1e-05) * gains).astype(jnp.bfloat16)
    normed = normed_ref[:, pl.ds(offset, width)]
    query_width = query_ref.shape[1]
    key_width = key_ref.shape[1]
    out_ref[:, :query_width] = jnp.dot(normed, query_ref[...], preferred_element_type=jnp.float32)
    out_ref[:, query_width : query_width + key_width] = jnp.dot(
        normed, key_ref[...], preferred_element_type=jnp.float32
    )
    out_ref[:, query_width + key_width :] = jnp.dot(
        normed, value_ref[...], preferred_element_type=jnp.float32
    )


def partial_projection(block, hidden, gain, query_weight, key_weight, value_weight, gate, up, down):
    rows, features = hidden.shape
    width = query_weight.shape[0]
    total = query_weight.shape[1] + key_weight.shape[1] + value_weight.shape[1]
    slab_shape = (gate.shape[0] + down.shape[0], gate.shape[1] + up.shape[1])
    vmem = pl.BlockSpec(memory_space=pltpu.VMEM)
    return pl.pallas_call(
        projection_kernel,
        out_shape=(
            jax.ShapeDtypeStruct((rows, total), jnp.float32),
            jax.ShapeDtypeStruct(slab_shape, gate.dtype),
        ),
        in_specs=[pl.BlockSpec(memory_space=pltpu.SMEM)] + [vmem] * 8,
        out_specs=(vmem, vmem),
        scratch_shapes=[pltpu.VMEM((rows, features), jnp.bfloat16)],
        cost_estimate=pl.CostEstimate(
            flops=2 * rows * width * total,
            bytes_accessed=2 * (rows * features + features + width * total)
            + 4 * rows * total
            + 4 * slab_shape[0] * slab_shape[1],
            transcendentals=rows,
        ),
    )(block, hidden, gain, query_weight, key_weight, value_weight, gate, up, down)


def gathered_sum(x, axis):
    return jnp.sum(lax.all_gather(x, axis), axis=0)


def gather_by_exchange(x, axes):
    count = 1
    for axis in axes:
        count *= lax.axis_size(axis)
    copies = jnp.broadcast_to(x[None], (count,) + x.shape)
    return lax.all_to_all(copies, axes, 0, 0, tiled=True)


def per_device(
    hidden,
    lengths,
    attention_gain,
    query_weight,
    key_weight,
    value_weight,
    cached_keys,
    cached_values,
    output_weight,
    feedforward_gain,
    gate_weight,
    up_weight,
    down_weight,
):
    requests = hidden.shape[0]
    stream = hidden.astype(jnp.float32)
    query_width = query_weight.shape[1]
    key_width = key_weight.shape[1]
    slab_rows, hidden_units = gate_weight.shape
    with jax.named_scope("qkv_projection"):
        block = lax.axis_index("seq").astype(jnp.int32).reshape(1)
        partial, slab = partial_projection(
            block,
            hidden,
            attention_gain,
            query_weight,
            key_weight,
            value_weight,
            gate_weight,
            up_weight,
            down_weight,
        )
    with jax.named_scope("mlp_weight_gather"):
        blocks = lax.all_gather(slab, "mlp")
    slabs = blocks.shape[0]
    gate_full = blocks[:, :slab_rows, :hidden_units].reshape(slabs * slab_rows, hidden_units)
    up_full = blocks[:, :slab_rows, hidden_units:].reshape(slabs * slab_rows, hidden_units)
    down_blocks = blocks[:, slab_rows:, :]
    with jax.named_scope("qkv_projection"):
        total = gathered_sum(partial, "seq")
    queries_raw = total[:, :query_width]
    keys_raw = total[:, query_width : query_width + key_width]
    values_raw = total[:, query_width + key_width :]
    local_heads = query_width // HD
    key_heads = key_width // HD
    group_size = local_heads // key_heads
    queries = rotate(queries_raw.reshape(requests, local_heads, HD), lengths).astype(jnp.bfloat16)
    new_keys = (
        rotate(keys_raw.reshape(requests, key_heads, HD), lengths)
        .reshape(requests, key_heads * HD)
        .astype(jnp.bfloat16)
    )
    new_values = values_raw.astype(jnp.bfloat16)
    grouped = queries.reshape(requests, key_heads, group_size, HD)
    block_span = cached_keys.shape[1]
    score_scale = HD ** (-0.5)
    first_position = lax.axis_index("seq") * block_span
    positions = first_position + jnp.arange(block_span, dtype=jnp.int32)
    valid_mask = (positions[None, :] < lengths[:, None])[:, None, :]
    own_head = jnp.arange(key_heads)[:, None] == jnp.arange(key_heads)[None, :]
    with jax.named_scope("local_attention"):
        padded_queries = jnp.where(
            own_head[None, :, None, :, None],
            grouped[:, :, :, None, :],
            jnp.zeros((), grouped.dtype),
        ).reshape(requests, key_heads * group_size, key_heads * HD)
        scores = (
            jnp.einsum(
                "rmk,rpk->rmp", padded_queries, cached_keys, preferred_element_type=jnp.float32
            )
            * score_scale
        )
        block_max = jnp.max(jnp.where(valid_mask, scores, -1e30), axis=-1)
        exp_weights = jnp.where(valid_mask, jnp.exp(scores - block_max[..., None]), 0.0)
        block_sum = jnp.sum(exp_weights, axis=-1)
        every_head_acc = jnp.einsum(
            "rmp,rpk->rmk",
            exp_weights.astype(jnp.bfloat16),
            cached_values,
            preferred_element_type=jnp.float32,
        ).reshape(requests, key_heads * group_size, key_heads, HD)
        own_block = jnp.repeat(own_head, group_size, axis=0)
        block_acc = jnp.sum(jnp.where(own_block[None, :, :, None], every_head_acc, 0.0), axis=2)
    with jax.named_scope("softmax_merge"):
        state = jnp.concatenate([block_max[..., None], block_sum[..., None], block_acc], axis=-1)
        every_state = lax.all_gather(state, "seq")
        every_max = every_state[..., 0]
        every_sum = every_state[..., 1]
        every_acc = every_state[..., 2:]
        query_float = grouped.astype(jnp.float32).reshape(requests, local_heads, HD)
        head_keys = jnp.repeat(
            new_keys.astype(jnp.float32).reshape(requests, key_heads, HD), group_size, axis=1
        )
        head_values = jnp.repeat(
            new_values.astype(jnp.float32).reshape(requests, key_heads, HD), group_size, axis=1
        )
        self_score = jnp.sum(query_float * head_keys, axis=-1) * score_scale
        overall_max = jnp.maximum(jnp.max(every_max, axis=0), self_score)
        rescale = jnp.exp(every_max - overall_max[None])
        self_weight = jnp.exp(self_score - overall_max)
        total_weight = jnp.sum(every_sum * rescale, axis=0) + self_weight
        weighted_sum = (
            jnp.sum(every_acc * rescale[..., None], axis=0) + self_weight[..., None] * head_values
        )
        attended = (
            (weighted_sum / total_weight[..., None])
            .reshape(requests, local_heads * HD)
            .astype(jnp.bfloat16)
        )
    with jax.named_scope("output_projection"):
        partial_output = jnp.dot(attended, output_weight, preferred_element_type=jnp.float32)
        every_partial = gather_by_exchange(partial_output.astype(jnp.bfloat16), ("seq", "tp"))
        column_blocks = lax.axis_size("seq")
        projected = (
            every_partial.reshape(column_blocks, lax.axis_size("tp"), requests, -1)
            .astype(jnp.float32)
            .sum(axis=1)
            .astype(jnp.bfloat16)
            .transpose(1, 0, 2)
            .reshape(requests, -1)
        )
    mixed_stream = stream + projected.astype(jnp.float32)
    mlp_input = rms_norm(mixed_stream, feedforward_gain).astype(jnp.bfloat16)
    with jax.named_scope("feed_forward"):
        gate = jnp.dot(mlp_input, gate_full, preferred_element_type=jnp.float32)
        upward = jnp.dot(mlp_input, up_full, preferred_element_type=jnp.float32)
        activated = (jax.nn.silu(gate) * upward).astype(jnp.bfloat16)
        down_part = jnp.einsum(
            "rh,jhc->rjc", activated, down_blocks, preferred_element_type=jnp.float32
        ).reshape(requests, slabs * slab_rows)
    with jax.named_scope("down_reduction"):
        reducers = lax.axis_size("seq") * lax.axis_size("tp")
        pieces = down_part.reshape(requests, reducers, -1).transpose(1, 0, 2)
        own_piece = (
            lax.all_to_all(pieces.astype(jnp.bfloat16), ("seq", "tp"), 0, 0, tiled=True)
            .astype(jnp.float32)
            .sum(axis=0)
        )
        every_piece = gather_by_exchange(own_piece.astype(jnp.bfloat16), ("seq", "tp"))
        down_total = every_piece.transpose(1, 0, 2).reshape(requests, -1)
    updated_hidden = (mixed_stream + down_total.astype(jnp.float32)).astype(jnp.bfloat16)
    return (updated_hidden, new_keys, new_values)


def solution(mesh):
    return jax.shard_map(
        per_device,
        mesh=mesh,
        in_specs=(
            P("mlp", None),
            P("mlp"),
            P(),
            P("seq", "tp"),
            P("seq", "tp"),
            P("seq", "tp"),
            P("mlp", "seq", "tp"),
            P("mlp", "seq", "tp"),
            P("tp", "seq"),
            P(),
            P("mlp", ("seq", "tp")),
            P("mlp", ("seq", "tp")),
            P(("seq", "tp"), "mlp"),
        ),
        out_specs=(P("mlp", None), P("mlp", "tp"), P("mlp", "tp")),
        check_vma=False,
    )
```

```python
import jax
import jax.numpy as jnp
from jax import lax
from jax.experimental import pallas as pl
from jax.experimental.pallas import tpu as pltpu
from jax.sharding import PartitionSpec as P

HD = 64


def rms_norm(vectors, weights):
    mean_square = jnp.mean(vectors * vectors, axis=-1, keepdims=True)
    return vectors * lax.rsqrt(mean_square + 1e-05) * weights.astype(jnp.float32)


def rotate(vectors, positions):
    half_dim = vectors.shape[-1] // 2
    inverse = 500000.0 ** (-(jnp.arange(half_dim, dtype=jnp.float32) * 2.0 / vectors.shape[-1]))
    angles = positions.astype(jnp.float32)[:, None] * inverse[None, :]
    cosine = jnp.cos(angles)[:, None, :]
    sine_part = jnp.sin(angles)[:, None, :]
    first_half = vectors[..., :half_dim]
    second_half = vectors[..., half_dim:]
    return jnp.concatenate(
        [
            first_half * cosine - second_half * sine_part,
            second_half * cosine + first_half * sine_part,
        ],
        axis=-1,
    )


def projection_kernel(
    block_ref,
    hidden_ref,
    gain_ref,
    query_ref,
    key_ref,
    value_ref,
    gate_ref,
    up_ref,
    down_ref,
    out_ref,
    slab_ref,
    normed_ref,
):
    slab_rows, hidden_units = gate_ref.shape
    slab_ref[:slab_rows, :hidden_units] = gate_ref[...]
    slab_ref[:slab_rows, hidden_units:] = up_ref[...]
    slab_ref[slab_rows:, :] = down_ref[...]
    width = query_ref.shape[0]
    offset = pl.multiple_of(block_ref[0] * width, width)
    stream = hidden_ref[...].astype(jnp.float32)
    mean_square = jnp.mean(stream * stream, axis=-1, keepdims=True)
    gains = gain_ref[...].astype(jnp.float32)[None, :]
    normed_ref[...] = (stream * lax.rsqrt(mean_square + 1e-05) * gains).astype(jnp.bfloat16)
    normed = normed_ref[:, pl.ds(offset, width)]
    query_width = query_ref.shape[1]
    key_width = key_ref.shape[1]
    out_ref[:, :query_width] = jnp.dot(normed, query_ref[...], preferred_element_type=jnp.float32)
    out_ref[:, query_width : query_width + key_width] = jnp.dot(
        normed, key_ref[...], preferred_element_type=jnp.float32
    )
    out_ref[:, query_width + key_width :] = jnp.dot(
        normed, value_ref[...], preferred_element_type=jnp.float32
    )


def partial_projection(block, hidden, gain, query_weight, key_weight, value_weight, gate, up, down):
    rows, features = hidden.shape
    width = query_weight.shape[0]
    total = query_weight.shape[1] + key_weight.shape[1] + value_weight.shape[1]
    slab_shape = (gate.shape[0] + down.shape[0], gate.shape[1] + up.shape[1])
    vmem = pl.BlockSpec(memory_space=pltpu.VMEM)
    return pl.pallas_call(
        projection_kernel,
        out_shape=(
            jax.ShapeDtypeStruct((rows, total), jnp.float32),
            jax.ShapeDtypeStruct(slab_shape, gate.dtype),
        ),
        in_specs=[pl.BlockSpec(memory_space=pltpu.SMEM)] + [vmem] * 8,
        out_specs=(vmem, vmem),
        scratch_shapes=[pltpu.VMEM((rows, features), jnp.bfloat16)],
        cost_estimate=pl.CostEstimate(
            flops=2 * rows * width * total,
            bytes_accessed=2 * (rows * features + features + width * total)
            + 4 * rows * total
            + 4 * slab_shape[0] * slab_shape[1],
            transcendentals=rows,
        ),
    )(block, hidden, gain, query_weight, key_weight, value_weight, gate, up, down)


def gathered_sum(x, axis):
    return jnp.sum(lax.all_gather(x, axis), axis=0)


def gather_by_exchange(x, axes):
    count = 1
    for axis in axes:
        count *= lax.axis_size(axis)
    copies = jnp.broadcast_to(x[None], (count,) + x.shape)
    return lax.all_to_all(copies, axes, 0, 0, tiled=True)


def per_device(
    hidden,
    lengths,
    attention_gain,
    query_weight,
    key_weight,
    value_weight,
    cached_keys,
    cached_values,
    output_weight,
    feedforward_gain,
    gate_weight,
    up_weight,
    down_weight,
):
    requests = hidden.shape[0]
    stream = hidden.astype(jnp.float32)
    query_width = query_weight.shape[1]
    key_width = key_weight.shape[1]
    slab_rows, hidden_units = gate_weight.shape
    with jax.named_scope("qkv_projection"):
        block = lax.axis_index("seq").astype(jnp.int32).reshape(1)
        partial, slab = partial_projection(
            block,
            hidden,
            attention_gain,
            query_weight,
            key_weight,
            value_weight,
            gate_weight,
            up_weight,
            down_weight,
        )
    with jax.named_scope("mlp_weight_gather"):
        blocks = lax.all_gather(slab, "mlp")
    slabs = blocks.shape[0]
    gate_full = blocks[:, :slab_rows, :hidden_units].reshape(slabs * slab_rows, hidden_units)
    up_full = blocks[:, :slab_rows, hidden_units:].reshape(slabs * slab_rows, hidden_units)
    down_blocks = blocks[:, slab_rows:, :]
    with jax.named_scope("qkv_projection"):
        total = gathered_sum(partial, "seq")
    queries_raw = total[:, :query_width]
    keys_raw = total[:, query_width : query_width + key_width]
    values_raw = total[:, query_width + key_width :]
    local_heads = query_width // HD
    key_heads = key_width // HD
    group_size = local_heads // key_heads
    queries = rotate(queries_raw.reshape(requests, local_heads, HD), lengths).astype(jnp.bfloat16)
    new_keys = (
        rotate(keys_raw.reshape(requests, key_heads, HD), lengths)
        .reshape(requests, key_heads * HD)
        .astype(jnp.bfloat16)
    )
    new_values = values_raw.astype(jnp.bfloat16)
    grouped = queries.reshape(requests, key_heads, group_size, HD)
    block_span = cached_keys.shape[1]
    key_blocks = cached_keys.reshape(requests, block_span, key_heads, HD)
    value_blocks = cached_values.reshape(requests, block_span, key_heads, HD)
    score_scale = HD ** (-0.5)
    first_position = lax.axis_index("seq") * block_span
    positions = first_position + jnp.arange(block_span, dtype=jnp.int32)
    valid_mask = (positions[None, :] < lengths[:, None])[:, None, None, :]
    with jax.named_scope("local_attention"):
        scores = (
            jnp.einsum("rgqd,rpgd->rgqp", grouped, key_blocks, preferred_element_type=jnp.float32)
            * score_scale
        )
        block_max = jnp.max(jnp.where(valid_mask, scores, -1e30), axis=-1)
        exp_weights = jnp.where(valid_mask, jnp.exp(scores - block_max[..., None]), 0.0)
        block_sum = jnp.sum(exp_weights, axis=-1)
        block_acc = jnp.einsum(
            "rgqp,rpgd->rgqd",
            exp_weights.astype(jnp.bfloat16),
            value_blocks,
            preferred_element_type=jnp.float32,
        )
    with jax.named_scope("softmax_merge"):
        state = jnp.concatenate([block_max[..., None], block_sum[..., None], block_acc], axis=-1)
        every_state = lax.all_gather(state, "seq")
        every_max = every_state[..., 0]
        every_sum = every_state[..., 1]
        every_acc = every_state[..., 2:]
        query_float = grouped.astype(jnp.float32)
        self_score = (
            jnp.sum(
                query_float * new_keys.astype(jnp.float32).reshape(requests, key_heads, 1, HD),
                axis=-1,
            )
            * score_scale
        )
        overall_max = jnp.maximum(jnp.max(every_max, axis=0), self_score)
        rescale = jnp.exp(every_max - overall_max[None])
        self_weight = jnp.exp(self_score - overall_max)
        total_weight = jnp.sum(every_sum * rescale, axis=0) + self_weight
        weighted_sum = jnp.sum(every_acc * rescale[..., None], axis=0) + self_weight[
            ..., None
        ] * new_values.astype(jnp.float32).reshape(requests, key_heads, 1, HD)
        attended = (
            (weighted_sum / total_weight[..., None])
            .reshape(requests, local_heads * HD)
            .astype(jnp.bfloat16)
        )
    with jax.named_scope("output_projection"):
        partial_output = jnp.dot(attended, output_weight, preferred_element_type=jnp.float32)
        every_partial = gather_by_exchange(partial_output.astype(jnp.bfloat16), ("seq", "tp"))
        column_blocks = lax.axis_size("seq")
        projected = (
            every_partial.reshape(column_blocks, lax.axis_size("tp"), requests, -1)
            .astype(jnp.float32)
            .sum(axis=1)
            .astype(jnp.bfloat16)
            .transpose(1, 0, 2)
            .reshape(requests, -1)
        )
    mixed_stream = stream + projected.astype(jnp.float32)
    mlp_input = rms_norm(mixed_stream, feedforward_gain).astype(jnp.bfloat16)
    with jax.named_scope("feed_forward"):
        gate = jnp.dot(mlp_input, gate_full, preferred_element_type=jnp.float32)
        upward = jnp.dot(mlp_input, up_full, preferred_element_type=jnp.float32)
        activated = (jax.nn.silu(gate) * upward).astype(jnp.bfloat16)
        down_part = jnp.einsum(
            "rh,jhc->rjc", activated, down_blocks, preferred_element_type=jnp.float32
        ).reshape(requests, slabs * slab_rows)
    with jax.named_scope("down_reduction"):
        reducers = lax.axis_size("seq") * lax.axis_size("tp")
        lanes = 128
        pieces = (
            down_part.reshape(requests, reducers, -1)
            .transpose(1, 0, 2)
            .reshape(reducers, -1, lanes)
            .astype(jnp.bfloat16)
        )
        own_piece = (
            lax.all_to_all(pieces, ("seq", "tp"), 0, 0, tiled=True)
            .astype(jnp.float32)
            .sum(axis=0)
        )
        every_piece = gather_by_exchange(own_piece.astype(jnp.bfloat16), ("seq", "tp"))
        down_total = (
            every_piece.reshape(reducers, requests, -1).transpose(1, 0, 2).reshape(requests, -1)
        )
    updated_hidden = (mixed_stream + down_total.astype(jnp.float32)).astype(jnp.bfloat16)
    return (updated_hidden, new_keys, new_values)


def solution(mesh):
    return jax.shard_map(
        per_device,
        mesh=mesh,
        in_specs=(
            P("mlp", None),
            P("mlp"),
            P(),
            P("seq", "tp"),
            P("seq", "tp"),
            P("seq", "tp"),
            P("mlp", "seq", "tp"),
            P("mlp", "seq", "tp"),
            P("tp", "seq"),
            P(),
            P("mlp", ("seq", "tp")),
            P("mlp", ("seq", "tp")),
            P(("seq", "tp"), "mlp"),
        ),
        out_specs=(P("mlp", None), P("mlp", "tp"), P("mlp", "tp")),
        check_vma=False,
    )
```

```python
import jax
import jax.numpy as jnp
from jax import lax
from jax.experimental import pallas as pl
from jax.experimental.pallas import tpu as pltpu
from jax.sharding import PartitionSpec as P

HD = 64


def rms_norm(vectors, weights):
    mean_square = jnp.mean(vectors * vectors, axis=-1, keepdims=True)
    return vectors * lax.rsqrt(mean_square + 1e-05) * weights.astype(jnp.float32)


def rotate(vectors, positions):
    half_dim = vectors.shape[-1] // 2
    inverse = 500000.0 ** (-(jnp.arange(half_dim, dtype=jnp.float32) * 2.0 / vectors.shape[-1]))
    angles = positions.astype(jnp.float32)[:, None] * inverse[None, :]
    cosine = jnp.cos(angles)[:, None, :]
    sine_part = jnp.sin(angles)[:, None, :]
    first_half = vectors[..., :half_dim]
    second_half = vectors[..., half_dim:]
    return jnp.concatenate(
        [
            first_half * cosine - second_half * sine_part,
            second_half * cosine + first_half * sine_part,
        ],
        axis=-1,
    )


def projection_kernel(
    block_ref,
    hidden_ref,
    gain_ref,
    query_ref,
    key_ref,
    value_ref,
    gate_ref,
    up_ref,
    down_ref,
    out_ref,
    slab_ref,
    normed_ref,
):
    slab_rows, hidden_units = gate_ref.shape
    slab_ref[:slab_rows, :hidden_units] = gate_ref[...]
    slab_ref[:slab_rows, hidden_units:] = up_ref[...]
    slab_ref[slab_rows:, :] = down_ref[...]
    width = query_ref.shape[0]
    offset = pl.multiple_of(block_ref[0] * width, width)
    stream = hidden_ref[...].astype(jnp.float32)
    mean_square = jnp.mean(stream * stream, axis=-1, keepdims=True)
    gains = gain_ref[...].astype(jnp.float32)[None, :]
    normed_ref[...] = (stream * lax.rsqrt(mean_square + 1e-05) * gains).astype(jnp.bfloat16)
    normed = normed_ref[:, pl.ds(offset, width)]
    query_width = query_ref.shape[1]
    key_width = key_ref.shape[1]
    out_ref[:, :query_width] = jnp.dot(normed, query_ref[...], preferred_element_type=jnp.float32)
    out_ref[:, query_width : query_width + key_width] = jnp.dot(
        normed, key_ref[...], preferred_element_type=jnp.float32
    )
    out_ref[:, query_width + key_width :] = jnp.dot(
        normed, value_ref[...], preferred_element_type=jnp.float32
    )


def partial_projection(block, hidden, gain, query_weight, key_weight, value_weight, gate, up, down):
    rows, features = hidden.shape
    width = query_weight.shape[0]
    total = query_weight.shape[1] + key_weight.shape[1] + value_weight.shape[1]
    slab_shape = (gate.shape[0] + down.shape[0], gate.shape[1] + up.shape[1])
    vmem = pl.BlockSpec(memory_space=pltpu.VMEM)
    return pl.pallas_call(
        projection_kernel,
        out_shape=(
            jax.ShapeDtypeStruct((rows, total), jnp.float32),
            jax.ShapeDtypeStruct(slab_shape, gate.dtype),
        ),
        in_specs=[pl.BlockSpec(memory_space=pltpu.SMEM)] + [vmem] * 8,
        out_specs=(vmem, vmem),
        scratch_shapes=[pltpu.VMEM((rows, features), jnp.bfloat16)],
        cost_estimate=pl.CostEstimate(
            flops=2 * rows * width * total,
            bytes_accessed=2 * (rows * features + features + width * total)
            + 4 * rows * total
            + 4 * slab_shape[0] * slab_shape[1],
            transcendentals=rows,
        ),
    )(block, hidden, gain, query_weight, key_weight, value_weight, gate, up, down)


def gathered_sum(x, axis):
    return jnp.sum(lax.all_gather(x, axis), axis=0)


def gather_by_exchange(x, axes):
    count = 1
    for axis in axes:
        count *= lax.axis_size(axis)
    copies = jnp.broadcast_to(x[None], (count,) + x.shape)
    return lax.all_to_all(copies, axes, 0, 0, tiled=True)


def per_device(
    hidden,
    lengths,
    attention_gain,
    query_weight,
    key_weight,
    value_weight,
    cached_keys,
    cached_values,
    output_weight,
    feedforward_gain,
    gate_weight,
    up_weight,
    down_weight,
):
    requests = hidden.shape[0]
    stream = hidden.astype(jnp.float32)
    query_width = query_weight.shape[1]
    key_width = key_weight.shape[1]
    slab_rows, hidden_units = gate_weight.shape
    with jax.named_scope("qkv_projection"):
        block = lax.axis_index("seq").astype(jnp.int32).reshape(1)
        partial, slab = partial_projection(
            block,
            hidden,
            attention_gain,
            query_weight,
            key_weight,
            value_weight,
            gate_weight,
            up_weight,
            down_weight,
        )
    with jax.named_scope("mlp_weight_gather"):
        blocks = lax.all_gather(slab, "mlp")
    slabs = blocks.shape[0]
    gate_full = blocks[:, :slab_rows, :hidden_units].reshape(slabs * slab_rows, hidden_units)
    up_full = blocks[:, :slab_rows, hidden_units:].reshape(slabs * slab_rows, hidden_units)
    down_blocks = blocks[:, slab_rows:, :]
    with jax.named_scope("qkv_projection"):
        total = gathered_sum(partial, "seq")
    queries_raw = total[:, :query_width]
    keys_raw = total[:, query_width : query_width + key_width]
    values_raw = total[:, query_width + key_width :]
    local_heads = query_width // HD
    key_heads = key_width // HD
    group_size = local_heads // key_heads
    queries = rotate(queries_raw.reshape(requests, local_heads, HD), lengths).astype(jnp.bfloat16)
    new_keys = (
        rotate(keys_raw.reshape(requests, key_heads, HD), lengths)
        .reshape(requests, key_heads * HD)
        .astype(jnp.bfloat16)
    )
    new_values = values_raw.astype(jnp.bfloat16)
    grouped = queries.reshape(requests, key_heads, group_size, HD)
    block_span = cached_keys.shape[1]
    key_blocks = cached_keys.reshape(requests, block_span, key_heads, HD)
    value_blocks = cached_values.reshape(requests, block_span, key_heads, HD)
    score_scale = HD ** (-0.5)
    first_position = lax.axis_index("seq") * block_span
    positions = first_position + jnp.arange(block_span, dtype=jnp.int32)
    valid_mask = (positions[None, :] < lengths[:, None])[:, None, None, :]
    with jax.named_scope("local_attention"):
        scores = (
            jnp.einsum("rgqd,rpgd->rgqp", grouped, key_blocks, preferred_element_type=jnp.float32)
            * score_scale
        )
        block_max = jnp.max(jnp.where(valid_mask, scores, -1e30), axis=-1)
        exp_weights = jnp.where(valid_mask, jnp.exp(scores - block_max[..., None]), 0.0)
        block_sum = jnp.sum(exp_weights, axis=-1)
        block_acc = jnp.einsum(
            "rgqp,rpgd->rgqd",
            exp_weights.astype(jnp.bfloat16),
            value_blocks,
            preferred_element_type=jnp.float32,
        )
    with jax.named_scope("softmax_merge"):
        state = jnp.concatenate([block_max[..., None], block_sum[..., None], block_acc], axis=-1)
        every_state = lax.all_gather(
            state.reshape(requests, local_heads, HD + 2), "seq"
        ).reshape((-1,) + state.shape)
        every_max = every_state[..., 0]
        every_sum = every_state[..., 1]
        every_acc = every_state[..., 2:]
        query_float = grouped.astype(jnp.float32)
        self_score = (
            jnp.sum(
                query_float * new_keys.astype(jnp.float32).reshape(requests, key_heads, 1, HD),
                axis=-1,
            )
            * score_scale
        )
        overall_max = jnp.maximum(jnp.max(every_max, axis=0), self_score)
        rescale = jnp.exp(every_max - overall_max[None])
        self_weight = jnp.exp(self_score - overall_max)
        total_weight = jnp.sum(every_sum * rescale, axis=0) + self_weight
        weighted_sum = jnp.sum(every_acc * rescale[..., None], axis=0) + self_weight[
            ..., None
        ] * new_values.astype(jnp.float32).reshape(requests, key_heads, 1, HD)
        attended = (
            (weighted_sum / total_weight[..., None])
            .reshape(requests, local_heads * HD)
            .astype(jnp.bfloat16)
        )
    with jax.named_scope("output_projection"):
        partial_output = jnp.dot(attended, output_weight, preferred_element_type=jnp.float32)
        every_partial = gather_by_exchange(partial_output.astype(jnp.bfloat16), ("seq", "tp"))
        column_blocks = lax.axis_size("seq")
        projected = (
            every_partial.reshape(column_blocks, lax.axis_size("tp"), requests, -1)
            .astype(jnp.float32)
            .sum(axis=1)
            .astype(jnp.bfloat16)
            .transpose(1, 0, 2)
            .reshape(requests, -1)
        )
    mixed_stream = stream + projected.astype(jnp.float32)
    mlp_input = rms_norm(mixed_stream, feedforward_gain).astype(jnp.bfloat16)
    with jax.named_scope("feed_forward"):
        gate = jnp.dot(mlp_input, gate_full, preferred_element_type=jnp.float32)
        upward = jnp.dot(mlp_input, up_full, preferred_element_type=jnp.float32)
        activated = (jax.nn.silu(gate) * upward).astype(jnp.bfloat16)
        down_part = jnp.einsum(
            "rh,jhc->rjc", activated, down_blocks, preferred_element_type=jnp.float32
        ).reshape(requests, slabs * slab_rows)
    with jax.named_scope("down_reduction"):
        reducers = lax.axis_size("seq") * lax.axis_size("tp")
        lanes = 128
        pieces = (
            down_part.reshape(requests, reducers, -1)
            .transpose(1, 0, 2)
            .reshape(reducers, -1, lanes)
            .astype(jnp.bfloat16)
        )
        own_piece = (
            lax.all_to_all(pieces, ("seq", "tp"), 0, 0, tiled=True)
            .astype(jnp.float32)
            .sum(axis=0)
        )
        every_piece = gather_by_exchange(own_piece.astype(jnp.bfloat16), ("seq", "tp"))
        down_total = (
            every_piece.reshape(reducers, requests, -1).transpose(1, 0, 2).reshape(requests, -1)
        )
    updated_hidden = (mixed_stream + down_total.astype(jnp.float32)).astype(jnp.bfloat16)
    return (updated_hidden, new_keys, new_values)


def solution(mesh):
    return jax.shard_map(
        per_device,
        mesh=mesh,
        in_specs=(
            P("mlp", None),
            P("mlp"),
            P(),
            P("seq", "tp"),
            P("seq", "tp"),
            P("seq", "tp"),
            P("mlp", "seq", "tp"),
            P("mlp", "seq", "tp"),
            P("tp", "seq"),
            P(),
            P("mlp", ("seq", "tp")),
            P("mlp", ("seq", "tp")),
            P(("seq", "tp"), "mlp"),
        ),
        out_specs=(P("mlp", None), P("mlp", "tp"), P("mlp", "tp")),
        check_vma=False,
    )
```

```python
import jax
import jax.numpy as jnp
from jax import lax
from jax.experimental import pallas as pl
from jax.experimental.pallas import tpu as pltpu
from jax.sharding import PartitionSpec as P

HD = 64


def rms_norm(vectors, weights):
    mean_square = jnp.mean(vectors * vectors, axis=-1, keepdims=True)
    return vectors * lax.rsqrt(mean_square + 1e-05) * weights.astype(jnp.float32)


def rotate(vectors, positions):
    half_dim = vectors.shape[-1] // 2
    inverse = 500000.0 ** (-(jnp.arange(half_dim, dtype=jnp.float32) * 2.0 / vectors.shape[-1]))
    angles = positions.astype(jnp.float32)[:, None] * inverse[None, :]
    cosine = jnp.cos(angles)[:, None, :]
    sine_part = jnp.sin(angles)[:, None, :]
    first_half = vectors[..., :half_dim]
    second_half = vectors[..., half_dim:]
    return jnp.concatenate(
        [
            first_half * cosine - second_half * sine_part,
            second_half * cosine + first_half * sine_part,
        ],
        axis=-1,
    )


def projection_kernel(
    block_ref,
    hidden_ref,
    gain_ref,
    query_ref,
    key_ref,
    value_ref,
    gate_ref,
    up_ref,
    down_ref,
    out_ref,
    slab_ref,
    normed_ref,
):
    slab_rows, hidden_units = gate_ref.shape
    slab_ref[:slab_rows, :hidden_units] = gate_ref[...]
    slab_ref[:slab_rows, hidden_units:] = up_ref[...]
    slab_ref[slab_rows:, :] = down_ref[...]
    width = query_ref.shape[0]
    offset = pl.multiple_of(block_ref[0] * width, width)
    stream = hidden_ref[...].astype(jnp.float32)
    mean_square = jnp.mean(stream * stream, axis=-1, keepdims=True)
    gains = gain_ref[...].astype(jnp.float32)[None, :]
    normed_ref[...] = (stream * lax.rsqrt(mean_square + 1e-05) * gains).astype(jnp.bfloat16)
    normed = normed_ref[:, pl.ds(offset, width)]
    query_width = query_ref.shape[1]
    key_width = key_ref.shape[1]
    out_ref[:, :query_width] = jnp.dot(normed, query_ref[...], preferred_element_type=jnp.float32)
    out_ref[:, query_width : query_width + key_width] = jnp.dot(
        normed, key_ref[...], preferred_element_type=jnp.float32
    )
    out_ref[:, query_width + key_width :] = jnp.dot(
        normed, value_ref[...], preferred_element_type=jnp.float32
    )


def partial_projection(block, hidden, gain, query_weight, key_weight, value_weight, gate, up, down):
    rows, features = hidden.shape
    width = query_weight.shape[0]
    total = query_weight.shape[1] + key_weight.shape[1] + value_weight.shape[1]
    slab_shape = (gate.shape[0] + down.shape[0], gate.shape[1] + up.shape[1])
    vmem = pl.BlockSpec(memory_space=pltpu.VMEM)
    return pl.pallas_call(
        projection_kernel,
        out_shape=(
            jax.ShapeDtypeStruct((rows, total), jnp.float32),
            jax.ShapeDtypeStruct(slab_shape, gate.dtype),
        ),
        in_specs=[pl.BlockSpec(memory_space=pltpu.SMEM)] + [vmem] * 8,
        out_specs=(vmem, vmem),
        scratch_shapes=[pltpu.VMEM((rows, features), jnp.bfloat16)],
        cost_estimate=pl.CostEstimate(
            flops=2 * rows * width * total,
            bytes_accessed=2 * (rows * features + features + width * total)
            + 4 * rows * total
            + 4 * slab_shape[0] * slab_shape[1],
            transcendentals=rows,
        ),
    )(block, hidden, gain, query_weight, key_weight, value_weight, gate, up, down)


def gathered_sum(x, axis):
    return jnp.sum(lax.all_gather(x, axis), axis=0)


def gather_by_exchange(x, axes):
    count = 1
    for axis in axes:
        count *= lax.axis_size(axis)
    copies = jnp.broadcast_to(x[None], (count,) + x.shape)
    return lax.all_to_all(copies, axes, 0, 0, tiled=True)


def per_device(
    hidden,
    lengths,
    attention_gain,
    query_weight,
    key_weight,
    value_weight,
    cached_keys,
    cached_values,
    output_weight,
    feedforward_gain,
    gate_weight,
    up_weight,
    down_weight,
):
    requests = hidden.shape[0]
    stream = hidden.astype(jnp.float32)
    query_width = query_weight.shape[1]
    key_width = key_weight.shape[1]
    slab_rows, hidden_units = gate_weight.shape
    with jax.named_scope("qkv_projection"):
        block = lax.axis_index("seq").astype(jnp.int32).reshape(1)
        partial, slab = partial_projection(
            block,
            hidden,
            attention_gain,
            query_weight,
            key_weight,
            value_weight,
            gate_weight,
            up_weight,
            down_weight,
        )
    with jax.named_scope("mlp_weight_gather"):
        blocks = lax.all_gather(slab, "mlp")
    slabs = blocks.shape[0]
    gate_full = blocks[:, :slab_rows, :hidden_units].reshape(slabs * slab_rows, hidden_units)
    up_full = blocks[:, :slab_rows, hidden_units:].reshape(slabs * slab_rows, hidden_units)
    down_blocks = blocks[:, slab_rows:, :]
    with jax.named_scope("qkv_projection"):
        total = gathered_sum(partial, "seq")
    queries_raw = total[:, :query_width]
    keys_raw = total[:, query_width : query_width + key_width]
    values_raw = total[:, query_width + key_width :]
    local_heads = query_width // HD
    key_heads = key_width // HD
    group_size = local_heads // key_heads
    queries = rotate(queries_raw.reshape(requests, local_heads, HD), lengths).astype(jnp.bfloat16)
    new_keys = (
        rotate(keys_raw.reshape(requests, key_heads, HD), lengths)
        .reshape(requests, key_heads * HD)
        .astype(jnp.bfloat16)
    )
    new_values = values_raw.astype(jnp.bfloat16)
    grouped = queries.reshape(requests, key_heads, group_size, HD)
    block_span = cached_keys.shape[1]
    key_blocks = cached_keys.reshape(requests, block_span, key_heads, HD)
    value_blocks = cached_values.reshape(requests, block_span, key_heads, HD)
    score_scale = HD ** (-0.5)
    first_position = lax.axis_index("seq") * block_span
    positions = first_position + jnp.arange(block_span, dtype=jnp.int32)
    valid_mask = (positions[None, :] < lengths[:, None])[:, None, None, :]
    with jax.named_scope("local_attention"):
        scores = (
            jnp.einsum("rgqd,rpgd->rgqp", grouped, key_blocks, preferred_element_type=jnp.float32)
            * score_scale
        )
        block_max = jnp.max(jnp.where(valid_mask, scores, -1e30), axis=-1)
        exp_weights = jnp.where(valid_mask, jnp.exp(scores - block_max[..., None]), 0.0)
        block_sum = jnp.sum(exp_weights, axis=-1)
        block_acc = jnp.einsum(
            "rgqp,rpgd->rgqd",
            exp_weights.astype(jnp.bfloat16),
            value_blocks,
            preferred_element_type=jnp.float32,
        )
    with jax.named_scope("softmax_merge"):
        state = jnp.concatenate([block_max[..., None], block_sum[..., None], block_acc], axis=-1)
        every_state = lax.all_gather(state, "seq")
        every_max = every_state[..., 0]
        every_sum = every_state[..., 1]
        every_acc = every_state[..., 2:]
        query_float = grouped.astype(jnp.float32)
        self_score = (
            jnp.sum(
                query_float * new_keys.astype(jnp.float32).reshape(requests, key_heads, 1, HD),
                axis=-1,
            )
            * score_scale
        )
        overall_max = jnp.maximum(jnp.max(every_max, axis=0), self_score)
        rescale = jnp.exp(every_max - overall_max[None])
        self_weight = jnp.exp(self_score - overall_max)
        total_weight = jnp.sum(every_sum * rescale, axis=0) + self_weight
        weighted_sum = jnp.sum(every_acc * rescale[..., None], axis=0) + self_weight[
            ..., None
        ] * new_values.astype(jnp.float32).reshape(requests, key_heads, 1, HD)
        attended = (
            (weighted_sum / total_weight[..., None])
            .reshape(requests, local_heads * HD)
            .astype(jnp.bfloat16)
        )
    with jax.named_scope("output_projection"):
        partial_output = jnp.dot(attended, output_weight, preferred_element_type=jnp.float32)
        every_partial = gather_by_exchange(partial_output.astype(jnp.bfloat16), ("seq", "tp"))
        column_blocks = lax.axis_size("seq")
        projected = (
            every_partial.reshape(column_blocks, lax.axis_size("tp"), requests, -1)
            .astype(jnp.float32)
            .sum(axis=1)
            .astype(jnp.bfloat16)
            .transpose(1, 0, 2)
            .reshape(requests, -1)
        )
    mixed_stream = stream + projected.astype(jnp.float32)
    mlp_input = rms_norm(mixed_stream, feedforward_gain).astype(jnp.bfloat16)
    with jax.named_scope("feed_forward"):
        gate = jnp.dot(mlp_input, gate_full, preferred_element_type=jnp.float32)
        upward = jnp.dot(mlp_input, up_full, preferred_element_type=jnp.float32)
        activated = (jax.nn.silu(gate) * upward).astype(jnp.bfloat16)
        down_part = jnp.einsum(
            "rh,jhc->rjc", activated, down_blocks, preferred_element_type=jnp.float32
        ).reshape(requests, slabs * slab_rows)
    with jax.named_scope("down_reduction"):
        reducers = lax.axis_size("seq") * lax.axis_size("tp")
        lanes = 128
        pieces = (
            down_part.reshape(requests, reducers, -1)
            .transpose(1, 0, 2)
            .reshape(reducers, -1, lanes)
            .astype(jnp.bfloat16)
        )
        own_piece = (
            lax.all_to_all(pieces, ("seq", "tp"), 0, 0, tiled=True)
            .astype(jnp.float32)
            .sum(axis=0)
        )
        piece_width = down_part.shape[1] // reducers
        me = lax.axis_index("seq") * lax.axis_size("tp") + lax.axis_index("tp")
        own_stream = lax.dynamic_slice_in_dim(mixed_stream, me * piece_width, piece_width, 1)
        own_down = own_piece.astype(jnp.bfloat16).reshape(requests, piece_width)
        own_updated = (own_stream + own_down.astype(jnp.float32)).astype(jnp.bfloat16)
        every_piece = gather_by_exchange(own_updated, ("seq", "tp"))
    updated_hidden = every_piece.transpose(1, 0, 2).reshape(requests, -1)
    return (updated_hidden, new_keys, new_values)


def solution(mesh):
    return jax.shard_map(
        per_device,
        mesh=mesh,
        in_specs=(
            P("mlp", None),
            P("mlp"),
            P(),
            P("seq", "tp"),
            P("seq", "tp"),
            P("seq", "tp"),
            P("mlp", "seq", "tp"),
            P("mlp", "seq", "tp"),
            P("tp", "seq"),
            P(),
            P("mlp", ("seq", "tp")),
            P("mlp", ("seq", "tp")),
            P(("seq", "tp"), "mlp"),
        ),
        out_specs=(P("mlp", None), P("mlp", "tp"), P("mlp", "tp")),
        check_vma=False,
    )
```
